32 devices in a mesh: lat: 4 (over y, x), lon: 8 (over z, core).
Axes of the slice: x: 2, y: 2, z: 4, core: 2. Of those that a mesh axis runs over, the one named last changes fastest.
Arguments:
- inputs: bfloat16 [32, 128, 1024], P('lat', 'lon'), may hold values from -24 to 24
- input_weight: bfloat16 [2, 1024, 1536], replicated, may hold values from -0.1875 to 0.1875
- output_weight: bfloat16 [2, 512, 1024], replicated, may hold values from -0.25 to 0.25
- norm_gain: float32 [2, 1024], replicated, may hold values from 0.1 to 1.9
- position_bias: float32 [2, 8, 49], replicated, may hold values from -6 to 260
- cotangent: bfloat16 [32, 128, 1024], P('lat', 'lon'), may hold values from -6 to 6
Outputs:
- output: bfloat16 [32, 128, 1024], P('lat', 'lon')
- input_grad: bfloat16 [32, 128, 1024], P('lat', 'lon')
- input_weight_grad: float32 [2, 1024, 1536], P(None, 'lon')
- output_weight_grad: float32 [2, 512, 1024], P(None, 'lon')
- norm_gain_grad: float32 [2, 1024], replicated
- position_bias_grad: float32 [2, 8, 49], replicated
The draws below stay inside these ranges and needn't reach their ends.
All inputs are finite; a program needn't handle non-finite values.
Results may differ from the reference program's by a relative error of at most 0.04.
Values may be sent and summed in bfloat16 or wider, within the bound.
No kernel may reach another device: no remote copies, remote signals or barrier semaphores. Data moves between devices by JAX's collectives and lax.ppermute only.
A program may use at most 128 MiB of HBM per device.

```python
import math
import jax
import jax.numpy as jnp
from jax import lax

D = 1024
HEADS = 8
HEAD_DIM = 64
WIN = 7
LAYERS = 2
NLAT = 32
NLON = 128


def draw_inputs(key, part):
    noise_key, row_key, column_key = jax.random.split(key, 3)
    noise = jnp.clip(jax.random.normal(noise_key, (NLAT, NLON, D), jnp.float32), -4.0, 4.0)
    row_scale = jnp.exp(jax.random.uniform(row_key, (NLAT, NLON, 1), jnp.float32, math.log(0.3), math.log(3.0)))
    column_scale = jnp.exp(jax.random.uniform(column_key, (1, 1, D), jnp.float32, math.log(0.5), math.log(2.0)))
    return (noise * row_scale * column_scale).astype(jnp.bfloat16)


def draw_position_bias(key, part):
    noise_key = jax.random.fold_in(key, 0)
    bias_shape = (LAYERS, HEADS, WIN * WIN)
    return jnp.clip(jax.random.normal(noise_key, bias_shape, jnp.float32), -6.0, 6.0)


def block_levels(own_key, shape, shards, smallest, largest):
    factor_of, own = 1.0, jax.random.fold_in(own_key, 6)
    for dim, shards_of in shards:
        draws = jnp.exp(jax.random.uniform(jax.random.fold_in(own, dim), (shards_of,), jnp.float32, smallest / len(shards), largest / len(shards)))
        factor_of = factor_of * jnp.repeat(draws, shape[dim] // shards_of).reshape([-1 if axis == dim else 1 for axis in range(len(shape))])
    return factor_of


def scatter_about(key, extent, deviation, reach, cuts=(), held_as=jnp.bfloat16):
    level = block_levels(key, extent, cuts, -0.22, 0.18) if cuts else 1.0
    array = jax.random.normal(key, extent, jnp.float32) * deviation * level
    return jnp.minimum(jnp.maximum(array, -reach), reach).astype(held_as)


def setup_inputs(seed: int = 0) -> dict:
    key_of = jax.random.split(jax.random.key(seed), 7)
    inputs = draw_inputs(jax.random.fold_in(key_of[6], 71), 0)
    input_weight = scatter_about(key_of[1], (LAYERS, D, 3 * HEADS * HEAD_DIM), D ** -0.5, 0.1875)
    output_weight = scatter_about(key_of[2], (LAYERS, HEADS * HEAD_DIM, D), (HEADS * HEAD_DIM) ** -0.5, 0.25)
    norm_gain = jnp.clip(1.0 + 0.18 * jax.random.normal(key_of[3], (LAYERS, D), jnp.float32), 0.1, 1.9)
    position_bias = draw_position_bias(jax.random.fold_in(key_of[6], 71), 0)
    cotangent = scatter_about(key_of[5], (NLAT, NLON, D), 1.0, 6.0, ((0, 4), (1, 8)))
    return {"inputs": inputs, "input_weight": input_weight, "output_weight": output_weight, "norm_gain": norm_gain, "position_bias": position_bias, "cotangent": cotangent}


eps = 1e-05

def offset_list():
    radius = WIN // 2
    return [(step_lat, step_lon) for step_lat in range(-radius, radius + 1) for step_lon in range(-radius, radius + 1)]

def layer_norm(wide_input, gain):
    row_mean = lax.optimization_barrier(jnp.mean(wide_input, axis=-1, keepdims=True))
    centred = wide_input - row_mean
    variance = lax.optimization_barrier(jnp.mean(centred * centred, axis=-1, keepdims=True))
    return centred * lax.rsqrt(variance + eps) * gain

def extend(field):
    radius = WIN // 2
    wrapped = jnp.concatenate([field[:, -radius:], field, field[:, :radius]], axis=1)
    return jnp.pad(wrapped, ((radius, radius), (0, 0), (0, 0)))

def fold_back(widened):
    radius = WIN // 2
    width_all = widened.shape[1] - 2 * radius
    inner = widened[radius:-radius, radius:radius + width_all]
    inner = inner.at[:, :radius].add(widened[radius:-radius, radius + width_all:])
    inner = inner.at[:, width_all - radius:].add(widened[radius:-radius, :radius])
    return inner

def neighbour(widened, step_lat, step_lon, tile_rows, tile_cols):
    radius = WIN // 2
    return widened[radius + step_lat:radius + step_lat + tile_rows, radius + step_lon:radius + step_lon + tile_cols]

def attend(queries, keys_wide, values_wide, bias, valid_rows):
    tile_rows, tile_cols = (queries.shape[0], queries.shape[1])
    radius = WIN // 2
    score_scale = HEAD_DIM ** (-0.5)
    query_heads = queries.reshape(tile_rows, tile_cols, HEADS, HEAD_DIM).astype(jnp.float32)
    per_offset = []
    key_mask = []
    for step_lat, step_lon in offset_list():
        key_slice = neighbour(keys_wide, step_lat, step_lon, tile_rows, tile_cols)
        key_slice = key_slice.reshape(tile_rows, tile_cols, HEADS, HEAD_DIM).astype(jnp.float32)
        per_offset.append(jnp.einsum('abhd,abhd->abh', query_heads, key_slice))
        key_mask.append(valid_rows[radius + step_lat:radius + step_lat + tile_rows])
    scores = jnp.stack(per_offset, axis=-1) * score_scale + bias
    key_mask = jnp.stack(key_mask, axis=-1)[:, None, None, :]
    masked = jnp.where(key_mask, scores, -jnp.inf)
    row_max = lax.optimization_barrier(jnp.max(masked, axis=-1, keepdims=True))
    weights_exp = jnp.exp(masked - row_max)
    attention = weights_exp / lax.optimization_barrier(jnp.sum(weights_exp, axis=-1, keepdims=True))
    probs_low = attention.astype(jnp.bfloat16)
    mixed = jnp.zeros((tile_rows, tile_cols, HEADS, HEAD_DIM), jnp.float32)
    for offset_idx, (step_lat, step_lon) in enumerate(offset_list()):
        value_slice = neighbour(values_wide, step_lat, step_lon, tile_rows, tile_cols)
        value_slice = value_slice.reshape(tile_rows, tile_cols, HEADS, HEAD_DIM).astype(jnp.float32)
        mixed = mixed + probs_low[..., offset_idx, None].astype(jnp.float32) * value_slice
    return (attention, probs_low, mixed.reshape(tile_rows, tile_cols, HEADS * HEAD_DIM).astype(jnp.bfloat16))

def reference(inputs, input_weight, output_weight, norm_gain, position_bias, cotangent):
    radius = WIN // 2
    inner_width = HEADS * HEAD_DIM
    score_scale = HEAD_DIM ** (-0.5)
    lat_total, lon_total = (inputs.shape[0], inputs.shape[1])
    global_rows = jnp.arange(lat_total + 2 * radius, dtype=jnp.int32) - radius
    valid_rows = (global_rows >= 0) & (global_rows < lat_total)
    stream = inputs
    stored = []
    for layer_idx in range(LAYERS):
        wide_input = stream.astype(jnp.float32)
        normed_wide, pullback = jax.vjp(layer_norm, wide_input, norm_gain[layer_idx])
        normed = normed_wide.astype(jnp.bfloat16)
        packed = jnp.dot(normed, input_weight[layer_idx], preferred_element_type=jnp.float32).astype(jnp.bfloat16)
        queries = packed[..., :inner_width]
        keys_wide = extend(packed[..., inner_width:2 * inner_width])
        values_wide = extend(packed[..., 2 * inner_width:])
        attention, probs_low, mixed = attend(queries, keys_wide, values_wide, position_bias[layer_idx], valid_rows)
        branch = jnp.dot(mixed, output_weight[layer_idx], preferred_element_type=jnp.float32)
        stored.append((pullback, normed, queries, keys_wide, values_wide, attention, probs_low, mixed))
        stream = (wide_input + branch).astype(jnp.bfloat16)
    output = stream
    upstream = cotangent
    packed_grads = [None] * LAYERS
    output_grads = [None] * LAYERS
    gain_grads = [None] * LAYERS
    bias_grads = [None] * LAYERS
    for layer_idx in reversed(range(LAYERS)):
        pullback, normed, queries, keys_wide, values_wide, attention, probs_low, mixed = stored[layer_idx]
        output_grads[layer_idx] = jnp.einsum('abi,abd->id', mixed.astype(jnp.float32), upstream.astype(jnp.float32))
        grad_mixed = jnp.dot(upstream, output_weight[layer_idx].T, preferred_element_type=jnp.float32).astype(jnp.bfloat16)
        grad_heads = grad_mixed.reshape(lat_total, lon_total, HEADS, HEAD_DIM).astype(jnp.float32)
        query_heads = queries.reshape(lat_total, lon_total, HEADS, HEAD_DIM).astype(jnp.float32)
        per_offset = []
        for step_lat, step_lon in offset_list():
            value_slice = neighbour(values_wide, step_lat, step_lon, lat_total, lon_total)
            value_slice = value_slice.reshape(lat_total, lon_total, HEADS, HEAD_DIM).astype(jnp.float32)
            per_offset.append(jnp.einsum('abhd,abhd->abh', grad_heads, value_slice))
        grad_probs = jnp.stack(per_offset, axis=-1)
        row_delta = lax.optimization_barrier(jnp.sum(attention * grad_probs, axis=-1, keepdims=True))
        grad_scores = attention * (grad_probs - row_delta)
        bias_grads[layer_idx] = lax.optimization_barrier(jnp.sum(grad_scores, axis=(0, 1)))
        scores_low = grad_scores.astype(jnp.bfloat16)
        grad_query = jnp.zeros((lat_total, lon_total, HEADS, HEAD_DIM), jnp.float32)
        keys_acc = jnp.zeros((lat_total + 2 * radius, lon_total + 2 * radius, HEADS, HEAD_DIM), jnp.float32)
        values_acc = jnp.zeros((lat_total + 2 * radius, lon_total + 2 * radius, HEADS, HEAD_DIM), jnp.float32)
        for offset_idx, (step_lat, step_lon) in enumerate(offset_list()):
            key_slice = neighbour(keys_wide, step_lat, step_lon, lat_total, lon_total)
            key_slice = key_slice.reshape(lat_total, lon_total, HEADS, HEAD_DIM).astype(jnp.float32)
            score_piece = scores_low[..., offset_idx, None].astype(jnp.float32)
            prob_piece = probs_low[..., offset_idx, None].astype(jnp.float32)
            grad_query = grad_query + score_piece * key_slice
            row_lo = radius + step_lat
            col_lo = radius + step_lon
            keys_acc = keys_acc.at[row_lo:row_lo + lat_total, col_lo:col_lo + lon_total].add(score_piece * query_heads)
            values_acc = values_acc.at[row_lo:row_lo + lat_total, col_lo:col_lo + lon_total].add(prob_piece * grad_heads)
        grad_keys = fold_back(keys_acc) * score_scale
        grad_values = fold_back(values_acc)
        grad_packed = jnp.concatenate([(grad_query * score_scale).reshape(lat_total, lon_total, inner_width), grad_keys.reshape(lat_total, lon_total, inner_width), grad_values.reshape(lat_total, lon_total, inner_width)], axis=-1).astype(jnp.bfloat16)
        packed_grads[layer_idx] = jnp.einsum('abd,abe->de', normed.astype(jnp.float32), grad_packed.astype(jnp.float32))
        grad_normed = jnp.dot(grad_packed, input_weight[layer_idx].T, preferred_element_type=jnp.float32)
        grad_wide, gain_grad = pullback(grad_normed)
        gain_grads[layer_idx] = gain_grad
        upstream = (upstream.astype(jnp.float32) + grad_wide).astype(jnp.bfloat16)
    return (output, upstream, jnp.stack(packed_grads), jnp.stack(output_grads), jnp.stack(gain_grads), jnp.stack(bias_grads))
```

```python
import jax
import jax.numpy as jnp
from jax import lax
from jax.sharding import PartitionSpec as P

HEADS = 8
HEAD_DIM = 64
WIN = 7
LAYERS = 2


eps = 1e-05


def extended(block, sides, width):
    for axis, dim in sides:
        count = lax.axis_size(axis)
        forward = [(i, i + 1) for i in range(count - 1)]
        forward.append((count - 1, 0))
        backward = [(target, source) for source, target in forward]
        low = lax.ppermute(
            lax.slice_in_dim(block, block.shape[dim] - width, None, axis=dim), axis, forward
        )
        high = lax.ppermute(lax.slice_in_dim(block, 0, width, axis=dim), axis, backward)
        block = jnp.concatenate([low, block, high], axis=dim)
    return block


def spread_sum(term):
    return lax.psum_scatter(
        term.astype(jnp.bfloat16), ("lon", "lat"), scatter_dimension=0, tiled=True
    )


def gather_lat(parts):
    flat = jnp.concatenate([part.reshape(1, -1) for part in parts], axis=1)
    whole = lax.all_gather(flat, "lat", axis=0, tiled=True)
    pieces = []
    start = 0
    for part in parts:
        size = part.size
        piece = whole[:, start : start + size].reshape((-1,) + part.shape[1:])
        pieces.append(piece.astype(jnp.float32))
        start += size
    return pieces


def layer_norm(wide_input, gain):
    row_mean = jnp.mean(wide_input, axis=-1, keepdims=True)
    centred = wide_input - row_mean
    variance = jnp.mean(centred * centred, axis=-1, keepdims=True)
    return centred * lax.rsqrt(variance + eps) * gain


def cell_coords(rows, cols, shift):
    row_ids = jnp.arange(rows, dtype=jnp.int32)[:, None] + jnp.zeros((1, cols), jnp.int32) + shift
    col_ids = jnp.arange(cols, dtype=jnp.int32)[None, :] + jnp.zeros((rows, 1), jnp.int32) + shift
    return (row_ids.reshape(-1), col_ids.reshape(-1))


def window_table(query_rows, query_cols, query_shift, key_rows, key_cols, key_shift):
    radius = WIN // 2
    query_i, query_j = cell_coords(query_rows, query_cols, query_shift)
    key_i, key_j = cell_coords(key_rows, key_cols, key_shift)
    offsets = jnp.arange(WIN * WIN, dtype=jnp.int32)
    step_lat = offsets // WIN - radius
    step_lon = offsets % WIN - radius
    match_lat = key_i[None, None, :] - query_i[:, None, None] == step_lat[None, :, None]
    match_lon = key_j[None, None, :] - query_j[:, None, None] == step_lon[None, :, None]
    return match_lat & match_lon


def attend(queries, keys_wide, values_wide, bias, allowed, table_full):
    tile_rows, tile_cols = (queries.shape[0], queries.shape[1])
    score_scale = HEAD_DIM ** (-0.5)
    cells = tile_rows * tile_cols
    query_heads = queries.reshape(cells, HEADS, HEAD_DIM)
    key_heads = keys_wide.reshape(-1, HEADS, HEAD_DIM)
    value_heads = values_wide.reshape(-1, HEADS, HEAD_DIM)
    raw = jnp.einsum("qhd,khd->hqk", query_heads, key_heads, preferred_element_type=jnp.float32)
    bias_dense = jnp.einsum("ho,qok->hqk", bias, table_full, precision=lax.Precision.HIGHEST)
    scores = raw * score_scale + bias_dense
    masked = jnp.where(allowed[None], scores, -jnp.inf)
    row_max = jnp.max(masked, axis=-1, keepdims=True)
    weights_exp = jnp.exp(masked - row_max)
    attention = weights_exp / jnp.sum(weights_exp, axis=-1, keepdims=True)
    probs_low = attention.astype(jnp.bfloat16)
    mixed = jnp.einsum("hqk,khd->qhd", probs_low, value_heads, preferred_element_type=jnp.float32)
    return (
        attention,
        probs_low,
        mixed.reshape(tile_rows, tile_cols, HEADS * HEAD_DIM).astype(jnp.bfloat16),
    )


def pull_back(received, back_table):
    inner_width = HEADS * HEAD_DIM
    spread = HEADS * WIN * WIN
    flat = received.reshape(-1, received.shape[-1])
    query_heads = flat[:, :inner_width].reshape(-1, HEADS, HEAD_DIM)
    grad_heads = flat[:, inner_width : 2 * inner_width].reshape(-1, HEADS, HEAD_DIM)
    prob_piece = flat[:, 2 * inner_width : 2 * inner_width + spread].reshape(-1, HEADS, WIN * WIN)
    score_piece = flat[:, 2 * inner_width + spread :].reshape(-1, HEADS, WIN * WIN)
    score_dense = jnp.einsum(
        "qho,qok->hqk", score_piece, back_table, preferred_element_type=jnp.float32
    ).astype(jnp.bfloat16)
    prob_dense = jnp.einsum(
        "qho,qok->hqk", prob_piece, back_table, preferred_element_type=jnp.float32
    ).astype(jnp.bfloat16)
    grad_keys = jnp.einsum(
        "hqk,qhd->khd", score_dense, query_heads, preferred_element_type=jnp.float32
    )
    grad_values = jnp.einsum(
        "hqk,qhd->khd", prob_dense, grad_heads, preferred_element_type=jnp.float32
    )
    return (grad_keys * HEAD_DIM ** (-0.5), grad_values)


def shards(inputs, input_weight, output_weight, norm_gain, position_bias, cotangent):
    radius = WIN // 2
    inner_width = HEADS * HEAD_DIM
    score_scale = HEAD_DIM ** (-0.5)
    tile_rows, tile_cols = (inputs.shape[0], inputs.shape[1])
    cells = tile_rows * tile_cols
    wide_rows = tile_rows + 2 * radius
    wide_cols = tile_cols + 2 * radius
    first_row = lax.axis_index("lat") * tile_rows - radius
    global_rows = first_row + jnp.arange(wide_rows, dtype=jnp.int32)
    valid_rows = (global_rows >= 0) & (global_rows < tile_rows * lax.axis_size("lat"))
    row_keep = valid_rows.astype(jnp.bfloat16)[:, None, None]
    key_valid = (valid_rows[:, None] & jnp.ones((1, wide_cols), jnp.bool_)).reshape(-1)
    forward_table = window_table(tile_rows, tile_cols, radius, wide_rows, wide_cols, 0)
    table_low = forward_table.astype(jnp.bfloat16)
    table_full = forward_table.astype(jnp.float32)
    allowed = jnp.any(forward_table, axis=1) & key_valid[None, :]
    back_table = window_table(wide_rows, wide_cols, 0, tile_rows, tile_cols, radius).astype(
        jnp.bfloat16
    )
    stream = inputs
    stored = []
    for layer_idx in range(LAYERS):
        wide_input = stream.astype(jnp.float32)
        normed_wide, pullback = jax.vjp(layer_norm, wide_input, norm_gain[layer_idx])
        normed = normed_wide.astype(jnp.bfloat16)
        packed = jnp.einsum(
            "abd,de->abe", normed, input_weight[layer_idx], preferred_element_type=jnp.float32
        ).astype(jnp.bfloat16)
        queries = packed[..., :inner_width]
        key_value = packed[..., inner_width:]
        pair_wide = extended(key_value, (("lat", 0), ("lon", 1)), radius)
        keys_wide = pair_wide[..., :inner_width]
        values_wide = pair_wide[..., inner_width:]
        attention, probs_low, mixed = attend(
            queries, keys_wide, values_wide, position_bias[layer_idx], allowed, table_full
        )
        branch = jnp.einsum(
            "abi,id->abd", mixed, output_weight[layer_idx], preferred_element_type=jnp.float32
        )
        stored.append(
            (pullback, normed, queries, keys_wide, values_wide, attention, probs_low, mixed)
        )
        stream = (wide_input + branch).astype(jnp.bfloat16)
    upstream = cotangent
    packed_terms = [None] * LAYERS
    output_terms = [None] * LAYERS
    gain_terms = [None] * LAYERS
    bias_terms = [None] * LAYERS
    for layer_idx in reversed(range(LAYERS)):
        pullback, normed, queries, keys_wide, values_wide, attention, probs_low, mixed = stored[
            layer_idx
        ]
        output_term = jnp.einsum("abi,abd->id", mixed, upstream, preferred_element_type=jnp.float32)
        output_terms[layer_idx] = spread_sum(output_term)
        grad_mixed = jnp.einsum(
            "abd,id->abi", upstream, output_weight[layer_idx], preferred_element_type=jnp.float32
        ).astype(jnp.bfloat16)
        grad_heads = grad_mixed.reshape(cells, HEADS, HEAD_DIM)
        key_heads = keys_wide.reshape(-1, HEADS, HEAD_DIM)
        value_heads = values_wide.reshape(-1, HEADS, HEAD_DIM)
        grad_probs = jnp.einsum(
            "qhd,khd->hqk", grad_heads, value_heads, preferred_element_type=jnp.float32
        )
        row_delta = jnp.sum(attention * grad_probs, axis=-1, keepdims=True)
        grad_scores = attention * (grad_probs - row_delta)
        bias_terms[layer_idx] = jnp.einsum(
            "hqk,qok->ho", grad_scores, table_full, precision=lax.Precision.HIGHEST
        )
        scores_low = grad_scores.astype(jnp.bfloat16)
        grad_query = jnp.einsum(
            "hqk,khd->qhd", scores_low, key_heads, preferred_element_type=jnp.float32
        )
        probs_offset = jnp.einsum(
            "hqk,qok->qho", probs_low, table_low, preferred_element_type=jnp.float32
        ).astype(jnp.bfloat16)
        scores_offset = jnp.einsum(
            "hqk,qok->qho", scores_low, table_low, preferred_element_type=jnp.float32
        ).astype(jnp.bfloat16)
        outgoing = jnp.concatenate(
            [
                queries,
                grad_mixed,
                probs_offset.reshape(tile_rows, tile_cols, HEADS * WIN * WIN),
                scores_offset.reshape(tile_rows, tile_cols, HEADS * WIN * WIN),
            ],
            axis=-1,
        )
        received = extended(outgoing, (("lat", 0), ("lon", 1)), radius) * row_keep
        grad_keys, grad_values = pull_back(received, back_table)
        grad_packed = jnp.concatenate(
            [
                (grad_query * score_scale).reshape(tile_rows, tile_cols, inner_width),
                grad_keys.reshape(tile_rows, tile_cols, inner_width),
                grad_values.reshape(tile_rows, tile_cols, inner_width),
            ],
            axis=-1,
        ).astype(jnp.bfloat16)
        packed_term = jnp.einsum(
            "abd,abe->de", normed, grad_packed, preferred_element_type=jnp.float32
        )
        grad_normed = jnp.einsum(
            "abe,de->abd", grad_packed, input_weight[layer_idx], preferred_element_type=jnp.float32
        )
        grad_wide, gain_term = pullback(grad_normed)
        gain_terms[layer_idx] = gain_term
        upstream = (upstream.astype(jnp.float32) + grad_wide).astype(jnp.bfloat16)
        packed_terms[layer_idx] = spread_sum(packed_term)
    gathered = gather_lat(packed_terms + output_terms)
    packed_grad = jnp.stack(gathered[:LAYERS])
    output_grad = jnp.stack(gathered[LAYERS:])
    stats = jnp.concatenate(
        [jnp.stack(gain_terms).reshape(-1), jnp.stack(bias_terms).reshape(-1)]
    )
    stats = lax.psum(lax.psum(stats, "lon"), "lat")
    gain_count = LAYERS * norm_gain.shape[-1]
    gain_grad = stats[:gain_count].reshape(norm_gain.shape)
    bias_grad = stats[gain_count:].reshape(position_bias.shape)
    return (stream, upstream, packed_grad, output_grad, gain_grad, bias_grad)


def solution(mesh):
    return jax.shard_map(
        shards,
        mesh=mesh,
        in_specs=(P("lat", "lon", None), P(), P(), P(), P(), P("lat", "lon", None)),
        out_specs=(
            P("lat", "lon", None),
            P("lat", "lon", None),
            P(None, "lon", None),
            P(None, "lon", None),
            P(),
            P(),
        ),
        check_vma=False,
    )
```

```python
import jax
import jax.numpy as jnp
from jax import lax
from jax.sharding import PartitionSpec as P

HEADS = 8
HEAD_DIM = 64
WIN = 7
LAYERS = 2


eps = 1e-05


def extended(block, sides, width):
    for axis, dim in sides:
        count = lax.axis_size(axis)
        forward = [(i, i + 1) for i in range(count - 1)]
        forward.append((count - 1, 0))
        backward = [(target, source) for source, target in forward]
        low = lax.ppermute(
            lax.slice_in_dim(block, block.shape[dim] - width, None, axis=dim), axis, forward
        )
        high = lax.ppermute(lax.slice_in_dim(block, 0, width, axis=dim), axis, backward)
        block = jnp.concatenate([low, block, high], axis=dim)
    return block


def lon_sum(rows, extra=None):
    count = lax.axis_size("lon")
    lanes = 128
    flat = rows.astype(jnp.bfloat16).reshape(count, -1, lanes)
    if extra is not None:
        width = -(-extra.shape[0] // lanes) * lanes
        padded = jnp.pad(extra.astype(jnp.bfloat16), (0, width - extra.shape[0]))
        copies = jnp.broadcast_to(padded.reshape(1, -1, lanes), (count, width // lanes, lanes))
        flat = jnp.concatenate([flat, copies], axis=1)
    return lax.psum_scatter(flat, "lon", scatter_dimension=0, tiled=True).reshape(-1)


def layer_norm(wide_input, gain):
    row_mean = jnp.mean(wide_input, axis=-1, keepdims=True)
    centred = wide_input - row_mean
    variance = jnp.mean(centred * centred, axis=-1, keepdims=True)
    return centred * lax.rsqrt(variance + eps) * gain


def cell_coords(rows, cols, shift):
    row_ids = jnp.arange(rows, dtype=jnp.int32)[:, None] + jnp.zeros((1, cols), jnp.int32) + shift
    col_ids = jnp.arange(cols, dtype=jnp.int32)[None, :] + jnp.zeros((rows, 1), jnp.int32) + shift
    return (row_ids.reshape(-1), col_ids.reshape(-1))


def window_table(query_rows, query_cols, query_shift, key_rows, key_cols, key_shift):
    radius = WIN // 2
    query_i, query_j = cell_coords(query_rows, query_cols, query_shift)
    key_i, key_j = cell_coords(key_rows, key_cols, key_shift)
    offsets = jnp.arange(WIN * WIN, dtype=jnp.int32)
    step_lat = offsets // WIN - radius
    step_lon = offsets % WIN - radius
    match_lat = key_i[None, None, :] - query_i[:, None, None] == step_lat[None, :, None]
    match_lon = key_j[None, None, :] - query_j[:, None, None] == step_lon[None, :, None]
    return match_lat & match_lon


def attend(queries, keys_wide, values_wide, bias, allowed, table_full):
    tile_rows, tile_cols = (queries.shape[0], queries.shape[1])
    score_scale = HEAD_DIM ** (-0.5)
    cells = tile_rows * tile_cols
    query_heads = queries.reshape(cells, HEADS, HEAD_DIM)
    key_heads = keys_wide.reshape(-1, HEADS, HEAD_DIM)
    value_heads = values_wide.reshape(-1, HEADS, HEAD_DIM)
    raw = jnp.einsum("qhd,khd->hqk", query_heads, key_heads, preferred_element_type=jnp.float32)
    bias_dense = jnp.einsum("ho,qok->hqk", bias, table_full, precision=lax.Precision.HIGHEST)
    scores = raw * score_scale + bias_dense
    masked = jnp.where(allowed[None], scores, -jnp.inf)
    row_max = jnp.max(masked, axis=-1, keepdims=True)
    weights_exp = jnp.exp(masked - row_max)
    attention = weights_exp / jnp.sum(weights_exp, axis=-1, keepdims=True)
    probs_low = attention.astype(jnp.bfloat16)
    mixed = jnp.einsum("hqk,khd->qhd", probs_low, value_heads, preferred_element_type=jnp.float32)
    return (
        attention,
        probs_low,
        mixed.reshape(tile_rows, tile_cols, HEADS * HEAD_DIM).astype(jnp.bfloat16),
    )


def pull_back(received, back_table):
    inner_width = HEADS * HEAD_DIM
    spread = HEADS * WIN * WIN
    flat = received.reshape(-1, received.shape[-1])
    query_heads = flat[:, :inner_width].reshape(-1, HEADS, HEAD_DIM)
    grad_heads = flat[:, inner_width : 2 * inner_width].reshape(-1, HEADS, HEAD_DIM)
    prob_piece = flat[:, 2 * inner_width : 2 * inner_width + spread].reshape(-1, HEADS, WIN * WIN)
    score_piece = flat[:, 2 * inner_width + spread :].reshape(-1, HEADS, WIN * WIN)
    score_dense = jnp.einsum(
        "qho,qok->hqk", score_piece, back_table, preferred_element_type=jnp.float32
    ).astype(jnp.bfloat16)
    prob_dense = jnp.einsum(
        "qho,qok->hqk", prob_piece, back_table, preferred_element_type=jnp.float32
    ).astype(jnp.bfloat16)
    grad_keys = jnp.einsum(
        "hqk,qhd->khd", score_dense, query_heads, preferred_element_type=jnp.float32
    )
    grad_values = jnp.einsum(
        "hqk,qhd->khd", prob_dense, grad_heads, preferred_element_type=jnp.float32
    )
    return (grad_keys * HEAD_DIM ** (-0.5), grad_values)


def shards(inputs, input_weight, output_weight, norm_gain, position_bias, cotangent):
    radius = WIN // 2
    inner_width = HEADS * HEAD_DIM
    score_scale = HEAD_DIM ** (-0.5)
    tile_rows, tile_cols = (inputs.shape[0], inputs.shape[1])
    cells = tile_rows * tile_cols
    wide_rows = tile_rows + 2 * radius
    wide_cols = tile_cols + 2 * radius
    first_row = lax.axis_index("lat") * tile_rows - radius
    global_rows = first_row + jnp.arange(wide_rows, dtype=jnp.int32)
    valid_rows = (global_rows >= 0) & (global_rows < tile_rows * lax.axis_size("lat"))
    row_keep = valid_rows.astype(jnp.bfloat16)[:, None, None]
    key_valid = (valid_rows[:, None] & jnp.ones((1, wide_cols), jnp.bool_)).reshape(-1)
    forward_table = window_table(tile_rows, tile_cols, radius, wide_rows, wide_cols, 0)
    table_low = forward_table.astype(jnp.bfloat16)
    table_full = forward_table.astype(jnp.float32)
    allowed = jnp.any(forward_table, axis=1) & key_valid[None, :]
    back_table = window_table(wide_rows, wide_cols, 0, tile_rows, tile_cols, radius).astype(
        jnp.bfloat16
    )
    stream = inputs
    stored = []
    for layer_idx in range(LAYERS):
        wide_input = stream.astype(jnp.float32)
        normed_wide, pullback = jax.vjp(layer_norm, wide_input, norm_gain[layer_idx])
        normed = normed_wide.astype(jnp.bfloat16)
        packed = jnp.einsum(
            "abd,de->abe", normed, input_weight[layer_idx], preferred_element_type=jnp.float32
        ).astype(jnp.bfloat16)
        queries = packed[..., :inner_width]
        key_value = packed[..., inner_width:]
        pair_wide = extended(key_value, (("lat", 0), ("lon", 1)), radius)
        keys_wide = pair_wide[..., :inner_width]
        values_wide = pair_wide[..., inner_width:]
        attention, probs_low, mixed = attend(
            queries, keys_wide, values_wide, position_bias[layer_idx], allowed, table_full
        )
        branch = jnp.einsum(
            "abi,id->abd", mixed, output_weight[layer_idx], preferred_element_type=jnp.float32
        )
        stored.append(
            (pullback, normed, queries, keys_wide, values_wide, attention, probs_low, mixed)
        )
        stream = (wide_input + branch).astype(jnp.bfloat16)
    upstream = cotangent
    packed_terms = [None] * LAYERS
    output_terms = [None] * LAYERS
    gain_terms = [None] * LAYERS
    bias_terms = [None] * LAYERS
    for layer_idx in reversed(range(LAYERS)):
        pullback, normed, queries, keys_wide, values_wide, attention, probs_low, mixed = stored[
            layer_idx
        ]
        output_term = jnp.einsum("abi,abd->id", mixed, upstream, preferred_element_type=jnp.float32)
        output_part = lon_sum(output_term)
        grad_mixed = jnp.einsum(
            "abd,id->abi", upstream, output_weight[layer_idx], preferred_element_type=jnp.float32
        ).astype(jnp.bfloat16)
        grad_heads = grad_mixed.reshape(cells, HEADS, HEAD_DIM)
        key_heads = keys_wide.reshape(-1, HEADS, HEAD_DIM)
        value_heads = values_wide.reshape(-1, HEADS, HEAD_DIM)
        grad_probs = jnp.einsum(
            "qhd,khd->hqk", grad_heads, value_heads, preferred_element_type=jnp.float32
        )
        row_delta = jnp.sum(attention * grad_probs, axis=-1, keepdims=True)
        grad_scores = attention * (grad_probs - row_delta)
        bias_terms[layer_idx] = jnp.einsum(
            "hqk,qok->ho", grad_scores, table_full, precision=lax.Precision.HIGHEST
        )
        scores_low = grad_scores.astype(jnp.bfloat16)
        grad_query = jnp.einsum(
            "hqk,khd->qhd", scores_low, key_heads, preferred_element_type=jnp.float32
        )
        probs_offset = jnp.einsum(
            "hqk,qok->qho", probs_low, table_low, preferred_element_type=jnp.float32
        ).astype(jnp.bfloat16)
        scores_offset = jnp.einsum(
            "hqk,qok->qho", scores_low, table_low, preferred_element_type=jnp.float32
        ).astype(jnp.bfloat16)
        outgoing = jnp.concatenate(
            [
                queries,
                grad_mixed,
                probs_offset.reshape(tile_rows, tile_cols, HEADS * WIN * WIN),
                scores_offset.reshape(tile_rows, tile_cols, HEADS * WIN * WIN),
            ],
            axis=-1,
        )
        received = extended(outgoing, (("lat", 0), ("lon", 1)), radius) * row_keep
        grad_keys, grad_values = pull_back(received, back_table)
        grad_packed = jnp.concatenate(
            [
                (grad_query * score_scale).reshape(tile_rows, tile_cols, inner_width),
                grad_keys.reshape(tile_rows, tile_cols, inner_width),
                grad_values.reshape(tile_rows, tile_cols, inner_width),
            ],
            axis=-1,
        ).astype(jnp.bfloat16)
        packed_term = jnp.einsum(
            "abd,abe->de", normed, grad_packed, preferred_element_type=jnp.float32
        )
        grad_normed = jnp.einsum(
            "abe,de->abd", grad_packed, input_weight[layer_idx], preferred_element_type=jnp.float32
        )
        grad_wide, gain_term = pullback(grad_normed)
        gain_terms[layer_idx] = gain_term
        upstream = (upstream.astype(jnp.float32) + grad_wide).astype(jnp.bfloat16)
        stats = jnp.concatenate([gain_term.reshape(-1), bias_terms[layer_idx].reshape(-1)])
        packed_part = lon_sum(packed_term, stats)
        summed = lax.psum(jnp.concatenate([output_part, packed_part]), "lat").astype(jnp.float32)
        out_size = output_part.shape[0]
        pack_size = packed_term.size // lax.axis_size("lon")
        output_terms[layer_idx] = summed[:out_size].reshape(-1, output_term.shape[1])
        packed_terms[layer_idx] = summed[out_size : out_size + pack_size].reshape(
            -1, packed_term.shape[1]
        )
        gain_count = gain_term.shape[0]
        gain_terms[layer_idx] = summed[out_size + pack_size : out_size + pack_size + gain_count]
        bias_start = out_size + pack_size + gain_count
        bias_terms[layer_idx] = summed[bias_start : bias_start + bias_terms[layer_idx].size].reshape(
            bias_terms[layer_idx].shape
        )
    packed_grad = jnp.stack(packed_terms)
    output_grad = jnp.stack(output_terms)
    gain_grad = jnp.stack(gain_terms)
    bias_grad = jnp.stack(bias_terms)
    return (stream, upstream, packed_grad, output_grad, gain_grad, bias_grad)


def solution(mesh):
    return jax.shard_map(
        shards,
        mesh=mesh,
        in_specs=(P("lat", "lon", None), P(), P(), P(), P(), P("lat", "lon", None)),
        out_specs=(
            P("lat", "lon", None),
            P("lat", "lon", None),
            P(None, "lon", None),
            P(None, "lon", None),
            P(),
            P(),
        ),
        check_vma=False,
    )
```

```python
import jax
import jax.numpy as jnp
from jax import lax
from jax.sharding import PartitionSpec as P

HEADS = 8
HEAD_DIM = 64
WIN = 7
LAYERS = 2


eps = 1e-05


def extended(block, sides, width):
    for axis, dim in sides:
        count = lax.axis_size(axis)
        forward = [(i, i + 1) for i in range(count - 1)]
        forward.append((count - 1, 0))
        backward = [(target, source) for source, target in forward]
        low = lax.ppermute(
            lax.slice_in_dim(block, block.shape[dim] - width, None, axis=dim), axis, forward
        )
        high = lax.ppermute(lax.slice_in_dim(block, 0, width, axis=dim), axis, backward)
        block = jnp.concatenate([low, block, high], axis=dim)
    return block


def lon_sum(rows, extra=None):
    count = lax.axis_size("lon")
    lanes = 128
    flat = rows.astype(jnp.bfloat16).reshape(count, -1, lanes)
    if extra is None:
        return lax.psum_scatter(flat, "lon", scatter_dimension=0, tiled=True).reshape(-1)
    width = -(-extra.shape[0] // lanes) * lanes
    padded = jnp.pad(extra.astype(jnp.bfloat16), (0, width - extra.shape[0]))
    copies = jnp.broadcast_to(padded.reshape(1, -1, lanes), (count, width // lanes, lanes))
    parts = lax.psum_scatter((flat, copies), "lon", scatter_dimension=0, tiled=True)
    return jnp.concatenate([part.reshape(-1) for part in parts])


def layer_norm(wide_input, gain):
    row_mean = jnp.mean(wide_input, axis=-1, keepdims=True)
    centred = wide_input - row_mean
    variance = jnp.mean(centred * centred, axis=-1, keepdims=True)
    return centred * lax.rsqrt(variance + eps) * gain


def cell_coords(rows, cols, shift):
    row_ids = jnp.arange(rows, dtype=jnp.int32)[:, None] + jnp.zeros((1, cols), jnp.int32) + shift
    col_ids = jnp.arange(cols, dtype=jnp.int32)[None, :] + jnp.zeros((rows, 1), jnp.int32) + shift
    return (row_ids.reshape(-1), col_ids.reshape(-1))


def window_table(query_rows, query_cols, query_shift, key_rows, key_cols, key_shift):
    radius = WIN // 2
    query_i, query_j = cell_coords(query_rows, query_cols, query_shift)
    key_i, key_j = cell_coords(key_rows, key_cols, key_shift)
    offsets = jnp.arange(WIN * WIN, dtype=jnp.int32)
    step_lat = offsets // WIN - radius
    step_lon = offsets % WIN - radius
    match_lat = key_i[None, None, :] - query_i[:, None, None] == step_lat[None, :, None]
    match_lon = key_j[None, None, :] - query_j[:, None, None] == step_lon[None, :, None]
    return match_lat & match_lon


def attend(queries, keys_wide, values_wide, bias, allowed, table_full):
    tile_rows, tile_cols = (queries.shape[0], queries.shape[1])
    score_scale = HEAD_DIM ** (-0.5)
    cells = tile_rows * tile_cols
    query_heads = queries.reshape(cells, HEADS, HEAD_DIM)
    key_heads = keys_wide.reshape(-1, HEADS, HEAD_DIM)
    value_heads = values_wide.reshape(-1, HEADS, HEAD_DIM)
    raw = jnp.einsum("qhd,khd->hqk", query_heads, key_heads, preferred_element_type=jnp.float32)
    bias_dense = jnp.einsum("ho,qok->hqk", bias, table_full, precision=lax.Precision.HIGHEST)
    scores = raw * score_scale + bias_dense
    masked = jnp.where(allowed[None], scores, -jnp.inf)
    row_max = jnp.max(masked, axis=-1, keepdims=True)
    weights_exp = jnp.exp(masked - row_max)
    attention = weights_exp / jnp.sum(weights_exp, axis=-1, keepdims=True)
    probs_low = attention.astype(jnp.bfloat16)
    mixed = jnp.einsum("hqk,khd->qhd", probs_low, value_heads, preferred_element_type=jnp.float32)
    return (
        attention,
        probs_low,
        mixed.reshape(tile_rows, tile_cols, HEADS * HEAD_DIM).astype(jnp.bfloat16),
    )


def pull_back(received, back_table):
    inner_width = HEADS * HEAD_DIM
    spread = HEADS * WIN * WIN
    flat = received.reshape(-1, received.shape[-1])
    query_heads = flat[:, :inner_width].reshape(-1, HEADS, HEAD_DIM)
    grad_heads = flat[:, inner_width : 2 * inner_width].reshape(-1, HEADS, HEAD_DIM)
    prob_piece = flat[:, 2 * inner_width : 2 * inner_width + spread].reshape(-1, HEADS, WIN * WIN)
    score_piece = flat[:, 2 * inner_width + spread :].reshape(-1, HEADS, WIN * WIN)
    score_dense = jnp.einsum(
        "qho,qok->hqk", score_piece, back_table, preferred_element_type=jnp.float32
    ).astype(jnp.bfloat16)
    prob_dense = jnp.einsum(
        "qho,qok->hqk", prob_piece, back_table, preferred_element_type=jnp.float32
    ).astype(jnp.bfloat16)
    grad_keys = jnp.einsum(
        "hqk,qhd->khd", score_dense, query_heads, preferred_element_type=jnp.float32
    )
    grad_values = jnp.einsum(
        "hqk,qhd->khd", prob_dense, grad_heads, preferred_element_type=jnp.float32
    )
    return (grad_keys * HEAD_DIM ** (-0.5), grad_values)


def shards(inputs, input_weight, output_weight, norm_gain, position_bias, cotangent):
    radius = WIN // 2
    inner_width = HEADS * HEAD_DIM
    score_scale = HEAD_DIM ** (-0.5)
    tile_rows, tile_cols = (inputs.shape[0], inputs.shape[1])
    cells = tile_rows * tile_cols
    wide_rows = tile_rows + 2 * radius
    wide_cols = tile_cols + 2 * radius
    first_row = lax.axis_index("lat") * tile_rows - radius
    global_rows = first_row + jnp.arange(wide_rows, dtype=jnp.int32)
    valid_rows = (global_rows >= 0) & (global_rows < tile_rows * lax.axis_size("lat"))
    row_keep = valid_rows.astype(jnp.bfloat16)[:, None, None]
    key_valid = (valid_rows[:, None] & jnp.ones((1, wide_cols), jnp.bool_)).reshape(-1)
    forward_table = window_table(tile_rows, tile_cols, radius, wide_rows, wide_cols, 0)
    table_low = forward_table.astype(jnp.bfloat16)
    table_full = forward_table.astype(jnp.float32)
    allowed = jnp.any(forward_table, axis=1) & key_valid[None, :]
    back_table = window_table(wide_rows, wide_cols, 0, tile_rows, tile_cols, radius).astype(
        jnp.bfloat16
    )
    stream = inputs
    stored = []
    for layer_idx in range(LAYERS):
        wide_input = stream.astype(jnp.float32)
        normed_wide, pullback = jax.vjp(layer_norm, wide_input, norm_gain[layer_idx])
        normed = normed_wide.astype(jnp.bfloat16)
        packed = jnp.einsum(
            "abd,de->abe", normed, input_weight[layer_idx], preferred_element_type=jnp.float32
        ).astype(jnp.bfloat16)
        queries = packed[..., :inner_width]
        key_value = packed[..., inner_width:]
        pair_wide = extended(key_value, (("lat", 0), ("lon", 1)), radius)
        keys_wide = pair_wide[..., :inner_width]
        values_wide = pair_wide[..., inner_width:]
        attention, probs_low, mixed = attend(
            queries, keys_wide, values_wide, position_bias[layer_idx], allowed, table_full
        )
        branch = jnp.einsum(
            "abi,id->abd", mixed, output_weight[layer_idx], preferred_element_type=jnp.float32
        )
        stored.append(
            (pullback, normed, queries, keys_wide, values_wide, attention, probs_low, mixed)
        )
        stream = (wide_input + branch).astype(jnp.bfloat16)
    upstream = cotangent
    previous = None
    done_terms = []
    packed_terms = [None] * LAYERS
    output_terms = [None] * LAYERS
    gain_terms = [None] * LAYERS
    bias_terms = [None] * LAYERS
    for layer_idx in reversed(range(LAYERS)):
        pullback, normed, queries, keys_wide, values_wide, attention, probs_low, mixed = stored[
            layer_idx
        ]
        output_term = jnp.einsum("abi,abd->id", mixed, upstream, preferred_element_type=jnp.float32)
        output_part = lon_sum(output_term)
        grad_mixed = jnp.einsum(
            "abd,id->abi", upstream, output_weight[layer_idx], preferred_element_type=jnp.float32
        ).astype(jnp.bfloat16)
        grad_heads = grad_mixed.reshape(cells, HEADS, HEAD_DIM)
        key_heads = keys_wide.reshape(-1, HEADS, HEAD_DIM)
        value_heads = values_wide.reshape(-1, HEADS, HEAD_DIM)
        grad_probs = jnp.einsum(
            "qhd,khd->hqk", grad_heads, value_heads, preferred_element_type=jnp.float32
        )
        row_delta = jnp.sum(attention * grad_probs, axis=-1, keepdims=True)
        grad_scores = attention * (grad_probs - row_delta)
        bias_terms[layer_idx] = jnp.einsum(
            "hqk,qok->ho", grad_scores, table_full, precision=lax.Precision.HIGHEST
        )
        scores_low = grad_scores.astype(jnp.bfloat16)
        grad_query = jnp.einsum(
            "hqk,khd->qhd", scores_low, key_heads, preferred_element_type=jnp.float32
        )
        probs_offset = jnp.einsum(
            "hqk,qok->qho", probs_low, table_low, preferred_element_type=jnp.float32
        ).astype(jnp.bfloat16)
        scores_offset = jnp.einsum(
            "hqk,qok->qho", scores_low, table_low, preferred_element_type=jnp.float32
        ).astype(jnp.bfloat16)
        outgoing = jnp.concatenate(
            [
                queries,
                grad_mixed,
                probs_offset.reshape(tile_rows, tile_cols, HEADS * WIN * WIN),
                scores_offset.reshape(tile_rows, tile_cols, HEADS * WIN * WIN),
            ],
            axis=-1,
        )
        received = extended(outgoing, (("lat", 0), ("lon", 1)), radius) * row_keep
        grad_keys, grad_values = pull_back(received, back_table)
        grad_packed = jnp.concatenate(
            [
                (grad_query * score_scale).reshape(tile_rows, tile_cols, inner_width),
                grad_keys.reshape(tile_rows, tile_cols, inner_width),
                grad_values.reshape(tile_rows, tile_cols, inner_width),
            ],
            axis=-1,
        ).astype(jnp.bfloat16)
        if previous is not None:
            previous, grad_packed = lax.optimization_barrier((previous, grad_packed))
            done_terms.append(previous)
        packed_term = jnp.einsum(
            "abd,abe->de", normed, grad_packed, preferred_element_type=jnp.float32
        )
        grad_normed = jnp.einsum(
            "abe,de->abd", grad_packed, input_weight[layer_idx], preferred_element_type=jnp.float32
        )
        grad_wide, gain_term = pullback(grad_normed)
        gain_terms[layer_idx] = gain_term
        upstream = (upstream.astype(jnp.float32) + grad_wide).astype(jnp.bfloat16)
        stats = jnp.concatenate([gain_term.reshape(-1), bias_terms[layer_idx].reshape(-1)])
        packed_part = lon_sum(packed_term, stats)
        payload = jnp.concatenate([output_part, packed_part])
        summed = lax.psum(payload, "lat")
        previous = summed
        summed = summed.astype(jnp.float32)
        out_size = output_part.shape[0]
        pack_size = packed_term.size // lax.axis_size("lon")
        output_terms[layer_idx] = summed[:out_size].reshape(-1, output_term.shape[1])
        packed_terms[layer_idx] = summed[out_size : out_size + pack_size].reshape(
            -1, packed_term.shape[1]
        )
        gain_count = gain_term.shape[0]
        gain_terms[layer_idx] = summed[out_size + pack_size : out_size + pack_size + gain_count]
        bias_start = out_size + pack_size + gain_count
        bias_terms[layer_idx] = summed[bias_start : bias_start + bias_terms[layer_idx].size].reshape(
            bias_terms[layer_idx].shape
        )
    packed_grad = jnp.stack(packed_terms)
    output_grad = jnp.stack(output_terms)
    gain_grad = jnp.stack(gain_terms)
    bias_grad = jnp.stack(bias_terms)
    return (stream, upstream, packed_grad, output_grad, gain_grad, bias_grad)


def solution(mesh):
    return jax.shard_map(
        shards,
        mesh=mesh,
        in_specs=(P("lat", "lon", None), P(), P(), P(), P(), P("lat", "lon", None)),
        out_specs=(
            P("lat", "lon", None),
            P("lat", "lon", None),
            P(None, "lon", None),
            P(None, "lon", None),
            P(),
            P(),
        ),
        check_vma=False,
    )
```

```python
import jax
import jax.numpy as jnp
from jax import lax
from jax.sharding import PartitionSpec as P

HEADS = 8
HEAD_DIM = 64
WIN = 7
LAYERS = 2


eps = 1e-05


def extended(block, sides, width):
    for axis, dim in sides:
        count = lax.axis_size(axis)
        forward = [(i, i + 1) for i in range(count - 1)]
        forward.append((count - 1, 0))
        backward = [(target, source) for source, target in forward]
        low = lax.ppermute(
            lax.slice_in_dim(block, block.shape[dim] - width, None, axis=dim), axis, forward
        )
        high = lax.ppermute(lax.slice_in_dim(block, 0, width, axis=dim), axis, backward)
        block = jnp.concatenate([low, block, high], axis=dim)
    return block


def lon_sum(rows, extra=None):
    count = lax.axis_size("lon")
    lanes = 128
    flat = rows.astype(jnp.bfloat16).reshape(count, -1, lanes)
    return lax.psum_scatter(flat, "lon", scatter_dimension=0, tiled=True).reshape(-1)


def doubling_sum(value, axis, keep):
    count = lax.axis_size(axis)
    step = 1
    total = value
    while step < count:
        pairs = [(i, i ^ step) for i in range(count)]
        other = lax.ppermute(total, axis, pairs)
        total = total.astype(jnp.float32) + other.astype(jnp.float32)
        step *= 2
        if step < count:
            total = total.astype(keep)
    return total


def layer_norm(wide_input, gain):
    row_mean = jnp.mean(wide_input, axis=-1, keepdims=True)
    centred = wide_input - row_mean
    variance = jnp.mean(centred * centred, axis=-1, keepdims=True)
    return centred * lax.rsqrt(variance + eps) * gain


def cell_coords(rows, cols, shift):
    row_ids = jnp.arange(rows, dtype=jnp.int32)[:, None] + jnp.zeros((1, cols), jnp.int32) + shift
    col_ids = jnp.arange(cols, dtype=jnp.int32)[None, :] + jnp.zeros((rows, 1), jnp.int32) + shift
    return (row_ids.reshape(-1), col_ids.reshape(-1))


def window_table(query_rows, query_cols, query_shift, key_rows, key_cols, key_shift):
    radius = WIN // 2
    query_i, query_j = cell_coords(query_rows, query_cols, query_shift)
    key_i, key_j = cell_coords(key_rows, key_cols, key_shift)
    offsets = jnp.arange(WIN * WIN, dtype=jnp.int32)
    step_lat = offsets // WIN - radius
    step_lon = offsets % WIN - radius
    match_lat = key_i[None, None, :] - query_i[:, None, None] == step_lat[None, :, None]
    match_lon = key_j[None, None, :] - query_j[:, None, None] == step_lon[None, :, None]
    return match_lat & match_lon


def attend(queries, keys_wide, values_wide, bias, allowed, table_full):
    tile_rows, tile_cols = (queries.shape[0], queries.shape[1])
    score_scale = HEAD_DIM ** (-0.5)
    cells = tile_rows * tile_cols
    query_heads = queries.reshape(cells, HEADS, HEAD_DIM)
    key_heads = keys_wide.reshape(-1, HEADS, HEAD_DIM)
    value_heads = values_wide.reshape(-1, HEADS, HEAD_DIM)
    raw = jnp.einsum("qhd,khd->hqk", query_heads, key_heads, preferred_element_type=jnp.float32)
    bias_dense = jnp.einsum("ho,qok->hqk", bias, table_full, precision=lax.Precision.HIGHEST)
    scores = raw * score_scale + bias_dense
    masked = jnp.where(allowed[None], scores, -jnp.inf)
    row_max = jnp.max(masked, axis=-1, keepdims=True)
    weights_exp = jnp.exp(masked - row_max)
    attention = weights_exp / jnp.sum(weights_exp, axis=-1, keepdims=True)
    probs_low = attention.astype(jnp.bfloat16)
    mixed = jnp.einsum("hqk,khd->qhd", probs_low, value_heads, preferred_element_type=jnp.float32)
    return (
        attention,
        probs_low,
        mixed.reshape(tile_rows, tile_cols, HEADS * HEAD_DIM).astype(jnp.bfloat16),
    )


def pull_back(received, back_table):
    inner_width = HEADS * HEAD_DIM
    spread = HEADS * WIN * WIN
    flat = received.reshape(-1, received.shape[-1])
    query_heads = flat[:, :inner_width].reshape(-1, HEADS, HEAD_DIM)
    grad_heads = flat[:, inner_width : 2 * inner_width].reshape(-1, HEADS, HEAD_DIM)
    prob_piece = flat[:, 2 * inner_width : 2 * inner_width + spread].reshape(-1, HEADS, WIN * WIN)
    score_piece = flat[:, 2 * inner_width + spread :].reshape(-1, HEADS, WIN * WIN)
    score_dense = jnp.einsum(
        "qho,qok->hqk", score_piece, back_table, preferred_element_type=jnp.float32
    ).astype(jnp.bfloat16)
    prob_dense = jnp.einsum(
        "qho,qok->hqk", prob_piece, back_table, preferred_element_type=jnp.float32
    ).astype(jnp.bfloat16)
    grad_keys = jnp.einsum(
        "hqk,qhd->khd", score_dense, query_heads, preferred_element_type=jnp.float32
    )
    grad_values = jnp.einsum(
        "hqk,qhd->khd", prob_dense, grad_heads, preferred_element_type=jnp.float32
    )
    return (grad_keys * HEAD_DIM ** (-0.5), grad_values)


def shards(inputs, input_weight, output_weight, norm_gain, position_bias, cotangent):
    radius = WIN // 2
    inner_width = HEADS * HEAD_DIM
    score_scale = HEAD_DIM ** (-0.5)
    tile_rows, tile_cols = (inputs.shape[0], inputs.shape[1])
    cells = tile_rows * tile_cols
    wide_rows = tile_rows + 2 * radius
    wide_cols = tile_cols + 2 * radius
    first_row = lax.axis_index("lat") * tile_rows - radius
    global_rows = first_row + jnp.arange(wide_rows, dtype=jnp.int32)
    valid_rows = (global_rows >= 0) & (global_rows < tile_rows * lax.axis_size("lat"))
    row_keep = valid_rows.astype(jnp.bfloat16)[:, None, None]
    key_valid = (valid_rows[:, None] & jnp.ones((1, wide_cols), jnp.bool_)).reshape(-1)
    forward_table = window_table(tile_rows, tile_cols, radius, wide_rows, wide_cols, 0)
    table_low = forward_table.astype(jnp.bfloat16)
    table_full = forward_table.astype(jnp.float32)
    allowed = jnp.any(forward_table, axis=1) & key_valid[None, :]
    back_table = window_table(wide_rows, wide_cols, 0, tile_rows, tile_cols, radius).astype(
        jnp.bfloat16
    )
    stream = inputs
    stored = []
    for layer_idx in range(LAYERS):
        wide_input = stream.astype(jnp.float32)
        normed_wide, pullback = jax.vjp(layer_norm, wide_input, norm_gain[layer_idx])
        normed = normed_wide.astype(jnp.bfloat16)
        packed = jnp.einsum(
            "abd,de->abe", normed, input_weight[layer_idx], preferred_element_type=jnp.float32
        ).astype(jnp.bfloat16)
        queries = packed[..., :inner_width]
        key_value = packed[..., inner_width:]
        pair_wide = extended(key_value, (("lat", 0), ("lon", 1)), radius)
        keys_wide = pair_wide[..., :inner_width]
        values_wide = pair_wide[..., inner_width:]
        attention, probs_low, mixed = attend(
            queries, keys_wide, values_wide, position_bias[layer_idx], allowed, table_full
        )
        branch = jnp.einsum(
            "abi,id->abd", mixed, output_weight[layer_idx], preferred_element_type=jnp.float32
        )
        stored.append(
            (pullback, normed, queries, keys_wide, values_wide, attention, probs_low, mixed)
        )
        stream = (wide_input + branch).astype(jnp.bfloat16)
    upstream = cotangent
    packed_terms = [None] * LAYERS
    output_terms = [None] * LAYERS
    gain_terms = [None] * LAYERS
    bias_terms = [None] * LAYERS
    for layer_idx in reversed(range(LAYERS)):
        pullback, normed, queries, keys_wide, values_wide, attention, probs_low, mixed = stored[
            layer_idx
        ]
        output_term = jnp.einsum("abi,abd->id", mixed, upstream, preferred_element_type=jnp.float32)
        output_part = lon_sum(output_term)
        grad_mixed = jnp.einsum(
            "abd,id->abi", upstream, output_weight[layer_idx], preferred_element_type=jnp.float32
        ).astype(jnp.bfloat16)
        grad_heads = grad_mixed.reshape(cells, HEADS, HEAD_DIM)
        key_heads = keys_wide.reshape(-1, HEADS, HEAD_DIM)
        value_heads = values_wide.reshape(-1, HEADS, HEAD_DIM)
        grad_probs = jnp.einsum(
            "qhd,khd->hqk", grad_heads, value_heads, preferred_element_type=jnp.float32
        )
        row_delta = jnp.sum(attention * grad_probs, axis=-1, keepdims=True)
        grad_scores = attention * (grad_probs - row_delta)
        bias_terms[layer_idx] = jnp.einsum(
            "hqk,qok->ho", grad_scores, table_full, precision=lax.Precision.HIGHEST
        )
        scores_low = grad_scores.astype(jnp.bfloat16)
        grad_query = jnp.einsum(
            "hqk,khd->qhd", scores_low, key_heads, preferred_element_type=jnp.float32
        )
        probs_offset = jnp.einsum(
            "hqk,qok->qho", probs_low, table_low, preferred_element_type=jnp.float32
        ).astype(jnp.bfloat16)
        scores_offset = jnp.einsum(
            "hqk,qok->qho", scores_low, table_low, preferred_element_type=jnp.float32
        ).astype(jnp.bfloat16)
        outgoing = jnp.concatenate(
            [
                queries,
                grad_mixed,
                probs_offset.reshape(tile_rows, tile_cols, HEADS * WIN * WIN),
                scores_offset.reshape(tile_rows, tile_cols, HEADS * WIN * WIN),
            ],
            axis=-1,
        )
        received = extended(outgoing, (("lat", 0), ("lon", 1)), radius) * row_keep
        grad_keys, grad_values = pull_back(received, back_table)
        grad_packed = jnp.concatenate(
            [
                (grad_query * score_scale).reshape(tile_rows, tile_cols, inner_width),
                grad_keys.reshape(tile_rows, tile_cols, inner_width),
                grad_values.reshape(tile_rows, tile_cols, inner_width),
            ],
            axis=-1,
        ).astype(jnp.bfloat16)
        packed_term = jnp.einsum(
            "abd,abe->de", normed, grad_packed, preferred_element_type=jnp.float32
        )
        grad_normed = jnp.einsum(
            "abe,de->abd", grad_packed, input_weight[layer_idx], preferred_element_type=jnp.float32
        )
        grad_wide, gain_term = pullback(grad_normed)
        gain_terms[layer_idx] = gain_term
        upstream = (upstream.astype(jnp.float32) + grad_wide).astype(jnp.bfloat16)
        packed_part = lon_sum(packed_term)
        summed = doubling_sum(jnp.concatenate([output_part, packed_part]), "lat", jnp.bfloat16)
        out_size = output_part.shape[0]
        output_terms[layer_idx] = summed[:out_size].reshape(-1, output_term.shape[1])
        packed_terms[layer_idx] = summed[out_size:].reshape(-1, packed_term.shape[1])
    stats = jnp.concatenate(
        [jnp.stack(gain_terms).reshape(-1), jnp.stack(bias_terms).reshape(-1)]
    )
    stats = doubling_sum(doubling_sum(stats, "lon", jnp.float32), "lat", jnp.float32)
    gain_count = LAYERS * norm_gain.shape[-1]
    gain_grad = stats[:gain_count].reshape(norm_gain.shape)
    bias_grad = stats[gain_count:].reshape(position_bias.shape)
    packed_grad = jnp.stack(packed_terms)
    output_grad = jnp.stack(output_terms)
    return (stream, upstream, packed_grad, output_grad, gain_grad, bias_grad)


def solution(mesh):
    return jax.shard_map(
        shards,
        mesh=mesh,
        in_specs=(P("lat", "lon", None), P(), P(), P(), P(), P("lat", "lon", None)),
        out_specs=(
            P("lat", "lon", None),
            P("lat", "lon", None),
            P(None, "lon", None),
            P(None, "lon", None),
            P(),
            P(),
        ),
        check_vma=False,
    )
```

```python
import jax
import jax.numpy as jnp
from jax import lax
from jax.sharding import PartitionSpec as P

HEADS = 8
HEAD_DIM = 64
WIN = 7
LAYERS = 2


eps = 1e-05


def extended(block, sides, width):
    for axis, dim in sides:
        count = lax.axis_size(axis)
        forward = [(i, i + 1) for i in range(count - 1)]
        forward.append((count - 1, 0))
        backward = [(target, source) for source, target in forward]
        low = lax.ppermute(
            lax.slice_in_dim(block, block.shape[dim] - width, None, axis=dim), axis, forward
        )
        high = lax.ppermute(lax.slice_in_dim(block, 0, width, axis=dim), axis, backward)
        block = jnp.concatenate([low, block, high], axis=dim)
    return block


def lon_sum(rows, extra=None):
    part = lax.psum_scatter(rows.astype(jnp.bfloat16), "lon", scatter_dimension=0, tiled=True)
    return part.reshape(-1)


def doubling_sum(value, axis, keep):
    count = lax.axis_size(axis)
    step = 1
    total = value
    while step < count:
        pairs = [(i, i ^ step) for i in range(count)]
        other = lax.ppermute(total, axis, pairs)
        total = total.astype(jnp.float32) + other.astype(jnp.float32)
        step *= 2
        if step < count:
            total = total.astype(keep)
    return total


def layer_norm(wide_input, gain):
    row_mean = jnp.mean(wide_input, axis=-1, keepdims=True)
    centred = wide_input - row_mean
    variance = jnp.mean(centred * centred, axis=-1, keepdims=True)
    return centred * lax.rsqrt(variance + eps) * gain


def cell_coords(rows, cols, shift):
    row_ids = jnp.arange(rows, dtype=jnp.int32)[:, None] + jnp.zeros((1, cols), jnp.int32) + shift
    col_ids = jnp.arange(cols, dtype=jnp.int32)[None, :] + jnp.zeros((rows, 1), jnp.int32) + shift
    return (row_ids.reshape(-1), col_ids.reshape(-1))


def window_table(query_rows, query_cols, query_shift, key_rows, key_cols, key_shift):
    radius = WIN // 2
    query_i, query_j = cell_coords(query_rows, query_cols, query_shift)
    key_i, key_j = cell_coords(key_rows, key_cols, key_shift)
    offsets = jnp.arange(WIN * WIN, dtype=jnp.int32)
    step_lat = offsets // WIN - radius
    step_lon = offsets % WIN - radius
    match_lat = key_i[None, None, :] - query_i[:, None, None] == step_lat[None, :, None]
    match_lon = key_j[None, None, :] - query_j[:, None, None] == step_lon[None, :, None]
    return match_lat & match_lon


def attend(queries, keys_wide, values_wide, bias, allowed, table_full):
    tile_rows, tile_cols = (queries.shape[0], queries.shape[1])
    score_scale = HEAD_DIM ** (-0.5)
    cells = tile_rows * tile_cols
    query_heads = queries.reshape(cells, HEADS, HEAD_DIM)
    key_heads = keys_wide.reshape(-1, HEADS, HEAD_DIM)
    value_heads = values_wide.reshape(-1, HEADS, HEAD_DIM)
    raw = jnp.einsum("qhd,khd->hqk", query_heads, key_heads, preferred_element_type=jnp.float32)
    bias_dense = jnp.einsum("ho,qok->hqk", bias, table_full, precision=lax.Precision.HIGHEST)
    scores = raw * score_scale + bias_dense
    masked = jnp.where(allowed[None], scores, -jnp.inf)
    row_max = jnp.max(masked, axis=-1, keepdims=True)
    weights_exp = jnp.exp(masked - row_max)
    attention = weights_exp / jnp.sum(weights_exp, axis=-1, keepdims=True)
    probs_low = attention.astype(jnp.bfloat16)
    mixed = jnp.einsum("hqk,khd->qhd", probs_low, value_heads, preferred_element_type=jnp.float32)
    return (
        attention,
        probs_low,
        mixed.reshape(tile_rows, tile_cols, HEADS * HEAD_DIM).astype(jnp.bfloat16),
    )


def pull_back(received, back_table):
    inner_width = HEADS * HEAD_DIM
    spread = HEADS * WIN * WIN
    flat = received.reshape(-1, received.shape[-1])
    query_heads = flat[:, :inner_width].reshape(-1, HEADS, HEAD_DIM)
    grad_heads = flat[:, inner_width : 2 * inner_width].reshape(-1, HEADS, HEAD_DIM)
    prob_piece = flat[:, 2 * inner_width : 2 * inner_width + spread].reshape(-1, HEADS, WIN * WIN)
    score_piece = flat[:, 2 * inner_width + spread :].reshape(-1, HEADS, WIN * WIN)
    score_dense = jnp.einsum(
        "qho,qok->hqk", score_piece, back_table, preferred_element_type=jnp.float32
    ).astype(jnp.bfloat16)
    prob_dense = jnp.einsum(
        "qho,qok->hqk", prob_piece, back_table, preferred_element_type=jnp.float32
    ).astype(jnp.bfloat16)
    grad_keys = jnp.einsum(
        "hqk,qhd->khd", score_dense, query_heads, preferred_element_type=jnp.float32
    )
    grad_values = jnp.einsum(
        "hqk,qhd->khd", prob_dense, grad_heads, preferred_element_type=jnp.float32
    )
    return (grad_keys * HEAD_DIM ** (-0.5), grad_values)


def shards(inputs, input_weight, output_weight, norm_gain, position_bias, cotangent):
    radius = WIN // 2
    inner_width = HEADS * HEAD_DIM
    score_scale = HEAD_DIM ** (-0.5)
    tile_rows, tile_cols = (inputs.shape[0], inputs.shape[1])
    cells = tile_rows * tile_cols
    wide_rows = tile_rows + 2 * radius
    wide_cols = tile_cols + 2 * radius
    first_row = lax.axis_index("lat") * tile_rows - radius
    global_rows = first_row + jnp.arange(wide_rows, dtype=jnp.int32)
    valid_rows = (global_rows >= 0) & (global_rows < tile_rows * lax.axis_size("lat"))
    row_keep = valid_rows.astype(jnp.bfloat16)[:, None, None]
    key_valid = (valid_rows[:, None] & jnp.ones((1, wide_cols), jnp.bool_)).reshape(-1)
    forward_table = window_table(tile_rows, tile_cols, radius, wide_rows, wide_cols, 0)
    table_low = forward_table.astype(jnp.bfloat16)
    table_full = forward_table.astype(jnp.float32)
    allowed = jnp.any(forward_table, axis=1) & key_valid[None, :]
    back_table = window_table(wide_rows, wide_cols, 0, tile_rows, tile_cols, radius).astype(
        jnp.bfloat16
    )
    stream = inputs
    stored = []
    for layer_idx in range(LAYERS):
        wide_input = stream.astype(jnp.float32)
        normed_wide, pullback = jax.vjp(layer_norm, wide_input, norm_gain[layer_idx])
        normed = normed_wide.astype(jnp.bfloat16)
        packed = jnp.einsum(
            "abd,de->abe", normed, input_weight[layer_idx], preferred_element_type=jnp.float32
        ).astype(jnp.bfloat16)
        queries = packed[..., :inner_width]
        key_value = packed[..., inner_width:]
        pair_wide = extended(key_value, (("lat", 0), ("lon", 1)), radius)
        keys_wide = pair_wide[..., :inner_width]
        values_wide = pair_wide[..., inner_width:]
        attention, probs_low, mixed = attend(
            queries, keys_wide, values_wide, position_bias[layer_idx], allowed, table_full
        )
        branch = jnp.einsum(
            "abi,id->abd", mixed, output_weight[layer_idx], preferred_element_type=jnp.float32
        )
        stored.append(
            (pullback, normed, queries, keys_wide, values_wide, attention, probs_low, mixed)
        )
        stream = (wide_input + branch).astype(jnp.bfloat16)
    upstream = cotangent
    previous = None
    done_terms = []
    packed_terms = [None] * LAYERS
    output_terms = [None] * LAYERS
    gain_terms = [None] * LAYERS
    bias_terms = [None] * LAYERS
    for layer_idx in reversed(range(LAYERS)):
        pullback, normed, queries, keys_wide, values_wide, attention, probs_low, mixed = stored[
            layer_idx
        ]
        output_term = jnp.einsum("abi,abd->id", mixed, upstream, preferred_element_type=jnp.float32)
        output_part = lon_sum(output_term)
        grad_mixed = jnp.einsum(
            "abd,id->abi", upstream, output_weight[layer_idx], preferred_element_type=jnp.float32
        ).astype(jnp.bfloat16)
        grad_heads = grad_mixed.reshape(cells, HEADS, HEAD_DIM)
        key_heads = keys_wide.reshape(-1, HEADS, HEAD_DIM)
        value_heads = values_wide.reshape(-1, HEADS, HEAD_DIM)
        grad_probs = jnp.einsum(
            "qhd,khd->hqk", grad_heads, value_heads, preferred_element_type=jnp.float32
        )
        row_delta = jnp.sum(attention * grad_probs, axis=-1, keepdims=True)
        grad_scores = attention * (grad_probs - row_delta)
        bias_terms[layer_idx] = jnp.einsum(
            "hqk,qok->ho", grad_scores, table_full, precision=lax.Precision.HIGHEST
        )
        scores_low = grad_scores.astype(jnp.bfloat16)
        grad_query = jnp.einsum(
            "hqk,khd->qhd", scores_low, key_heads, preferred_element_type=jnp.float32
        )
        probs_offset = jnp.einsum(
            "hqk,qok->qho", probs_low, table_low, preferred_element_type=jnp.float32
        ).astype(jnp.bfloat16)
        scores_offset = jnp.einsum(
            "hqk,qok->qho", scores_low, table_low, preferred_element_type=jnp.float32
        ).astype(jnp.bfloat16)
        outgoing = jnp.concatenate(
            [
                queries,
                grad_mixed,
                probs_offset.reshape(tile_rows, tile_cols, HEADS * WIN * WIN),
                scores_offset.reshape(tile_rows, tile_cols, HEADS * WIN * WIN),
            ],
            axis=-1,
        )
        received = extended(outgoing, (("lat", 0), ("lon", 1)), radius) * row_keep
        grad_keys, grad_values = pull_back(received, back_table)
        grad_packed = jnp.concatenate(
            [
                (grad_query * score_scale).reshape(tile_rows, tile_cols, inner_width),
                grad_keys.reshape(tile_rows, tile_cols, inner_width),
                grad_values.reshape(tile_rows, tile_cols, inner_width),
            ],
            axis=-1,
        ).astype(jnp.bfloat16)
        if previous is not None:
            previous, grad_packed = lax.optimization_barrier((previous, grad_packed))
            done_terms.append(previous)
        packed_term = jnp.einsum(
            "abd,abe->de", normed, grad_packed, preferred_element_type=jnp.float32
        )
        grad_normed = jnp.einsum(
            "abe,de->abd", grad_packed, input_weight[layer_idx], preferred_element_type=jnp.float32
        )
        grad_wide, gain_term = pullback(grad_normed)
        gain_terms[layer_idx] = gain_term
        upstream = (upstream.astype(jnp.float32) + grad_wide).astype(jnp.bfloat16)
        packed_part = lon_sum(packed_term)
        summed = doubling_sum(jnp.concatenate([output_part, packed_part]), "lat", jnp.bfloat16)
        out_size = output_part.shape[0]
        output_terms[layer_idx] = summed[:out_size].reshape(-1, output_term.shape[1])
        packed_terms[layer_idx] = summed[out_size:].reshape(-1, packed_term.shape[1])
        previous = summed
    stats = jnp.concatenate(
        [jnp.stack(gain_terms).reshape(-1), jnp.stack(bias_terms).reshape(-1)]
    )
    stats = doubling_sum(doubling_sum(stats, "lon", jnp.float32), "lat", jnp.float32)
    gain_count = LAYERS * norm_gain.shape[-1]
    gain_grad = stats[:gain_count].reshape(norm_gain.shape)
    bias_grad = stats[gain_count:].reshape(position_bias.shape)
    packed_grad = jnp.stack(packed_terms)
    output_grad = jnp.stack(output_terms)
    return (stream, upstream, packed_grad, output_grad, gain_grad, bias_grad)


def solution(mesh):
    return jax.shard_map(
        shards,
        mesh=mesh,
        in_specs=(P("lat", "lon", None), P(), P(), P(), P(), P("lat", "lon", None)),
        out_specs=(
            P("lat", "lon", None),
            P("lat", "lon", None),
            P(None, "lon", None),
            P(None, "lon", None),
            P(),
            P(),
        ),
        check_vma=False,
    )
```

```python
import jax
import jax.numpy as jnp
from jax import lax
from jax.sharding import PartitionSpec as P

HEADS = 8
HEAD_DIM = 64
WIN = 7
LAYERS = 2


eps = 1e-05


def extended(block, sides, width):
    for axis, dim in sides:
        count = lax.axis_size(axis)
        forward = [(i, i + 1) for i in range(count - 1)]
        forward.append((count - 1, 0))
        backward = [(target, source) for source, target in forward]
        low = lax.ppermute(
            lax.slice_in_dim(block, block.shape[dim] - width, None, axis=dim), axis, forward
        )
        high = lax.ppermute(lax.slice_in_dim(block, 0, width, axis=dim), axis, backward)
        block = jnp.concatenate([low, block, high], axis=dim)
    return block


def lon_sum(rows, extra=None):
    part = lax.psum_scatter(rows.astype(jnp.bfloat16), "lon", scatter_dimension=0, tiled=True)
    return part.reshape(-1)


def doubling_sum(value, axis, keep):
    count = lax.axis_size(axis)
    step = 1
    total = value
    while step < count:
        pairs = [(i, i ^ step) for i in range(count)]
        other = lax.ppermute(total, axis, pairs)
        total = total.astype(jnp.float32) + other.astype(jnp.float32)
        step *= 2
        if step < count:
            total = total.astype(keep)
    return total


def layer_norm(wide_input, gain):
    row_mean = jnp.mean(wide_input, axis=-1, keepdims=True)
    centred = wide_input - row_mean
    variance = jnp.mean(centred * centred, axis=-1, keepdims=True)
    return centred * lax.rsqrt(variance + eps) * gain


def cell_coords(rows, cols, shift):
    row_ids = jnp.arange(rows, dtype=jnp.int32)[:, None] + jnp.zeros((1, cols), jnp.int32) + shift
    col_ids = jnp.arange(cols, dtype=jnp.int32)[None, :] + jnp.zeros((rows, 1), jnp.int32) + shift
    return (row_ids.reshape(-1), col_ids.reshape(-1))


def window_table(query_rows, query_cols, query_shift, key_rows, key_cols, key_shift):
    radius = WIN // 2
    query_i, query_j = cell_coords(query_rows, query_cols, query_shift)
    key_i, key_j = cell_coords(key_rows, key_cols, key_shift)
    offsets = jnp.arange(WIN * WIN, dtype=jnp.int32)
    step_lat = offsets // WIN - radius
    step_lon = offsets % WIN - radius
    match_lat = key_i[None, None, :] - query_i[:, None, None] == step_lat[None, :, None]
    match_lon = key_j[None, None, :] - query_j[:, None, None] == step_lon[None, :, None]
    return match_lat & match_lon


def attend(queries, keys_wide, values_wide, bias, allowed, table_full):
    tile_rows, tile_cols = (queries.shape[0], queries.shape[1])
    score_scale = HEAD_DIM ** (-0.5)
    cells = tile_rows * tile_cols
    query_heads = queries.reshape(cells, HEADS, HEAD_DIM)
    key_heads = keys_wide.reshape(-1, HEADS, HEAD_DIM)
    value_heads = values_wide.reshape(-1, HEADS, HEAD_DIM)
    raw = jnp.einsum("qhd,khd->hqk", query_heads, key_heads, preferred_element_type=jnp.float32)
    bias_dense = jnp.einsum("ho,qok->hqk", bias, table_full, precision=lax.Precision.HIGHEST)
    scores = raw * score_scale + bias_dense
    masked = jnp.where(allowed[None], scores, -jnp.inf)
    row_max = jnp.max(masked, axis=-1, keepdims=True)
    weights_exp = jnp.exp(masked - row_max)
    attention = weights_exp / jnp.sum(weights_exp, axis=-1, keepdims=True)
    probs_low = attention.astype(jnp.bfloat16)
    mixed = jnp.einsum("hqk,khd->qhd", probs_low, value_heads, preferred_element_type=jnp.float32)
    return (
        attention,
        probs_low,
        mixed.reshape(tile_rows, tile_cols, HEADS * HEAD_DIM).astype(jnp.bfloat16),
    )


def pull_back(received, back_table):
    inner_width = HEADS * HEAD_DIM
    spread = HEADS * WIN * WIN
    flat = received.reshape(-1, received.shape[-1])
    query_heads = flat[:, :inner_width].reshape(-1, HEADS, HEAD_DIM)
    grad_heads = flat[:, inner_width : 2 * inner_width].reshape(-1, HEADS, HEAD_DIM)
    prob_piece = flat[:, 2 * inner_width : 2 * inner_width + spread].reshape(-1, HEADS, WIN * WIN)
    score_piece = flat[:, 2 * inner_width + spread :].reshape(-1, HEADS, WIN * WIN)
    score_dense = jnp.einsum(
        "qho,qok->hqk", score_piece, back_table, preferred_element_type=jnp.float32
    ).astype(jnp.bfloat16)
    prob_dense = jnp.einsum(
        "qho,qok->hqk", prob_piece, back_table, preferred_element_type=jnp.float32
    ).astype(jnp.bfloat16)
    grad_keys = jnp.einsum(
        "hqk,qhd->khd", score_dense, query_heads, preferred_element_type=jnp.float32
    )
    grad_values = jnp.einsum(
        "hqk,qhd->khd", prob_dense, grad_heads, preferred_element_type=jnp.float32
    )
    return (grad_keys * HEAD_DIM ** (-0.5), grad_values)


def shards(inputs, input_weight, output_weight, norm_gain, position_bias, cotangent):
    radius = WIN // 2
    inner_width = HEADS * HEAD_DIM
    score_scale = HEAD_DIM ** (-0.5)
    tile_rows, tile_cols = (inputs.shape[0], inputs.shape[1])
    cells = tile_rows * tile_cols
    wide_rows = tile_rows + 2 * radius
    wide_cols = tile_cols + 2 * radius
    first_row = lax.axis_index("lat") * tile_rows - radius
    global_rows = first_row + jnp.arange(wide_rows, dtype=jnp.int32)
    valid_rows = (global_rows >= 0) & (global_rows < tile_rows * lax.axis_size("lat"))
    row_keep = valid_rows.astype(jnp.bfloat16)[:, None, None]
    key_valid = (valid_rows[:, None] & jnp.ones((1, wide_cols), jnp.bool_)).reshape(-1)
    forward_table = window_table(tile_rows, tile_cols, radius, wide_rows, wide_cols, 0)
    table_low = forward_table.astype(jnp.bfloat16)
    table_full = forward_table.astype(jnp.float32)
    allowed = jnp.any(forward_table, axis=1) & key_valid[None, :]
    back_table = window_table(wide_rows, wide_cols, 0, tile_rows, tile_cols, radius).astype(
        jnp.bfloat16
    )
    stream = inputs
    stored = []
    for layer_idx in range(LAYERS):
        wide_input = stream.astype(jnp.float32)
        normed_wide, pullback = jax.vjp(layer_norm, wide_input, norm_gain[layer_idx])
        normed = normed_wide.astype(jnp.bfloat16)
        packed = jnp.einsum(
            "abd,de->abe", normed, input_weight[layer_idx], preferred_element_type=jnp.float32
        ).astype(jnp.bfloat16)
        queries = packed[..., :inner_width]
        key_value = packed[..., inner_width:]
        pair_wide = extended(key_value, (("lat", 0), ("lon", 1)), radius)
        keys_wide = pair_wide[..., :inner_width]
        values_wide = pair_wide[..., inner_width:]
        attention, probs_low, mixed = attend(
            queries, keys_wide, values_wide, position_bias[layer_idx], allowed, table_full
        )
        branch = jnp.einsum(
            "abi,id->abd", mixed, output_weight[layer_idx], preferred_element_type=jnp.float32
        )
        stored.append(
            (pullback, normed, queries, keys_wide, values_wide, attention, probs_low, mixed)
        )
        stream = (wide_input + branch).astype(jnp.bfloat16)
    upstream = cotangent
    packed_terms = [None] * LAYERS
    output_terms = [None] * LAYERS
    gain_terms = [None] * LAYERS
    bias_terms = [None] * LAYERS
    for layer_idx in reversed(range(LAYERS)):
        pullback, normed, queries, keys_wide, values_wide, attention, probs_low, mixed = stored[
            layer_idx
        ]
        output_term = jnp.einsum("abi,abd->id", mixed, upstream, preferred_element_type=jnp.float32)
        output_part = lon_sum(output_term)
        grad_mixed = jnp.einsum(
            "abd,id->abi", upstream, output_weight[layer_idx], preferred_element_type=jnp.float32
        ).astype(jnp.bfloat16)
        grad_heads = grad_mixed.reshape(cells, HEADS, HEAD_DIM)
        key_heads = keys_wide.reshape(-1, HEADS, HEAD_DIM)
        value_heads = values_wide.reshape(-1, HEADS, HEAD_DIM)
        grad_probs = jnp.einsum(
            "qhd,khd->hqk", grad_heads, value_heads, preferred_element_type=jnp.float32
        )
        row_delta = jnp.sum(attention * grad_probs, axis=-1, keepdims=True)
        grad_scores = attention * (grad_probs - row_delta)
        bias_terms[layer_idx] = jnp.einsum(
            "hqk,qok->ho", grad_scores, table_full, precision=lax.Precision.HIGHEST
        )
        scores_low = grad_scores.astype(jnp.bfloat16)
        grad_query = jnp.einsum(
            "hqk,khd->qhd", scores_low, key_heads, preferred_element_type=jnp.float32
        )
        probs_offset = jnp.einsum(
            "hqk,qok->qho", probs_low, table_low, preferred_element_type=jnp.float32
        ).astype(jnp.bfloat16)
        scores_offset = jnp.einsum(
            "hqk,qok->qho", scores_low, table_low, preferred_element_type=jnp.float32
        ).astype(jnp.bfloat16)
        outgoing = jnp.concatenate(
            [
                queries,
                grad_mixed,
                probs_offset.reshape(tile_rows, tile_cols, HEADS * WIN * WIN),
                scores_offset.reshape(tile_rows, tile_cols, HEADS * WIN * WIN),
            ],
            axis=-1,
        )
        received = extended(outgoing, (("lat", 0), ("lon", 1)), radius) * row_keep
        grad_keys, grad_values = pull_back(received, back_table)
        grad_packed = jnp.concatenate(
            [
                (grad_query * score_scale).reshape(tile_rows, tile_cols, inner_width),
                grad_keys.reshape(tile_rows, tile_cols, inner_width),
                grad_values.reshape(tile_rows, tile_cols, inner_width),
            ],
            axis=-1,
        ).astype(jnp.bfloat16)
        packed_term = jnp.einsum(
            "abd,abe->de", normed, grad_packed, preferred_element_type=jnp.float32
        )
        grad_normed = jnp.einsum(
            "abe,de->abd", grad_packed, input_weight[layer_idx], preferred_element_type=jnp.float32
        )
        grad_wide, gain_term = pullback(grad_normed)
        gain_terms[layer_idx] = gain_term
        upstream = (upstream.astype(jnp.float32) + grad_wide).astype(jnp.bfloat16)
        packed_part = lon_sum(packed_term)
        summed = doubling_sum(jnp.concatenate([output_part, packed_part]), "lat", jnp.bfloat16)
        out_size = output_part.shape[0]
        output_terms[layer_idx] = summed[:out_size].reshape(-1, output_term.shape[1])
        packed_terms[layer_idx] = summed[out_size:].reshape(-1, packed_term.shape[1])
    stats = jnp.concatenate(
        [jnp.stack(gain_terms).reshape(-1), jnp.stack(bias_terms).reshape(-1)]
    )
    stats = doubling_sum(doubling_sum(stats, "lon", jnp.float32), "lat", jnp.float32)
    gain_count = LAYERS * norm_gain.shape[-1]
    gain_grad = stats[:gain_count].reshape(norm_gain.shape)
    bias_grad = stats[gain_count:].reshape(position_bias.shape)
    packed_grad = jnp.stack(packed_terms)
    output_grad = jnp.stack(output_terms)
    return (stream, upstream, packed_grad, output_grad, gain_grad, bias_grad)


def solution(mesh):
    return jax.shard_map(
        shards,
        mesh=mesh,
        in_specs=(P("lat", "lon", None), P(), P(), P(), P(), P("lat", "lon", None)),
        out_specs=(
            P("lat", "lon", None),
            P("lat", "lon", None),
            P(None, "lon", None),
            P(None, "lon", None),
            P(),
            P(),
        ),
        check_vma=False,
    )
```

```python
import jax
import jax.numpy as jnp
from jax import lax
from jax.sharding import PartitionSpec as P

HEADS = 8
HEAD_DIM = 64
WIN = 7
LAYERS = 2


eps = 1e-05


def extended(block, sides, width):
    for axis, dim in sides:
        count = lax.axis_size(axis)
        forward = [(i, i + 1) for i in range(count - 1)]
        forward.append((count - 1, 0))
        backward = [(target, source) for source, target in forward]
        low = lax.ppermute(
            lax.slice_in_dim(block, block.shape[dim] - width, None, axis=dim), axis, forward
        )
        high = lax.ppermute(lax.slice_in_dim(block, 0, width, axis=dim), axis, backward)
        block = jnp.concatenate([low, block, high], axis=dim)
    return block


def lon_sum(rows, extra=None):
    part = lax.psum_scatter(rows.astype(jnp.bfloat16), "lon", scatter_dimension=0, tiled=True)
    return part.reshape(-1)


def doubling_sum(value, axis, keep):
    count = lax.axis_size(axis)
    step = 1
    total = value
    while step < count:
        pairs = [(i, i ^ step) for i in range(count)]
        other = lax.ppermute(total, axis, pairs)
        total = total.astype(jnp.float32) + other.astype(jnp.float32)
        step *= 2
        if step < count:
            total = total.astype(keep)
    return total


def layer_norm(wide_input, gain):
    row_mean = jnp.mean(wide_input, axis=-1, keepdims=True)
    centred = wide_input - row_mean
    variance = jnp.mean(centred * centred, axis=-1, keepdims=True)
    return centred * lax.rsqrt(variance + eps) * gain


def cell_coords(rows, cols, shift):
    row_ids = jnp.arange(rows, dtype=jnp.int32)[:, None] + jnp.zeros((1, cols), jnp.int32) + shift
    col_ids = jnp.arange(cols, dtype=jnp.int32)[None, :] + jnp.zeros((rows, 1), jnp.int32) + shift
    return (row_ids.reshape(-1), col_ids.reshape(-1))


def window_table(query_rows, query_cols, query_shift, key_rows, key_cols, key_shift):
    radius = WIN // 2
    query_i, query_j = cell_coords(query_rows, query_cols, query_shift)
    key_i, key_j = cell_coords(key_rows, key_cols, key_shift)
    offsets = jnp.arange(WIN * WIN, dtype=jnp.int32)
    step_lat = offsets // WIN - radius
    step_lon = offsets % WIN - radius
    match_lat = key_i[None, None, :] - query_i[:, None, None] == step_lat[None, :, None]
    match_lon = key_j[None, None, :] - query_j[:, None, None] == step_lon[None, :, None]
    return match_lat & match_lon


def toeplitz(values, rows, cols, wide):
    span = wide + 1
    lead = values.shape[:-1]
    padded = jnp.pad(values, [(0, 0)] * len(lead) + [(0, span - WIN)])
    tiled = jnp.broadcast_to(padded[..., None, :], lead + (rows, span)).reshape(lead + (rows * span,))
    return tiled[..., : rows * wide].reshape(lead + (rows, wide))

def skew(dense, rows, wide):
    span = wide + 1
    lead = dense.shape[:-2]
    flat = dense.reshape(lead + (rows * wide,))
    flat = jnp.pad(flat, [(0, 0)] * len(lead) + [(0, rows * span - rows * wide)])
    return flat.reshape(lead + (rows, span))[..., :WIN]

def bias_dense(bias, tr, tc):
    wr, wc = tr + WIN - 1, tc + WIN - 1
    b2 = bias.reshape(HEADS, WIN, WIN)
    along_cols = toeplitz(b2, tc, tc, wc)
    moved = jnp.moveaxis(along_cols, 1, -1)
    along_rows = toeplitz(moved, tr, tr, wr)
    return jnp.transpose(along_rows, (0, 3, 1, 4, 2)).reshape(HEADS, tr * tc, wr * wc)

def offset_sums(grad_scores, tr, tc):
    wr, wc = tr + WIN - 1, tc + WIN - 1
    g = grad_scores.reshape(HEADS, tr, tc, wr, wc)
    g = jnp.transpose(g, (0, 1, 3, 2, 4))
    by_w = skew(g, tc, wc).sum(axis=-2)
    by_w = jnp.transpose(by_w, (0, 3, 1, 2))
    by_uw = skew(by_w, tr, wr).sum(axis=-2)
    return jnp.transpose(by_uw, (0, 2, 1)).reshape(HEADS, WIN * WIN)

def attend(queries, keys_wide, values_wide, bias, allowed):
    tile_rows, tile_cols = (queries.shape[0], queries.shape[1])
    score_scale = HEAD_DIM ** (-0.5)
    cells = tile_rows * tile_cols
    query_heads = queries.reshape(cells, HEADS, HEAD_DIM)
    key_heads = keys_wide.reshape(-1, HEADS, HEAD_DIM)
    value_heads = values_wide.reshape(-1, HEADS, HEAD_DIM)
    raw = jnp.einsum("qhd,khd->hqk", query_heads, key_heads, preferred_element_type=jnp.float32)
    bias_wide = bias_dense(bias, tile_rows, tile_cols)
    scores = raw * score_scale + bias_wide
    masked = jnp.where(allowed[None], scores, -jnp.inf)
    row_max = jnp.max(masked, axis=-1, keepdims=True)
    weights_exp = jnp.exp(masked - row_max)
    attention = weights_exp / jnp.sum(weights_exp, axis=-1, keepdims=True)
    probs_low = attention.astype(jnp.bfloat16)
    mixed = jnp.einsum("hqk,khd->qhd", probs_low, value_heads, preferred_element_type=jnp.float32)
    return (
        attention,
        probs_low,
        mixed.reshape(tile_rows, tile_cols, HEADS * HEAD_DIM).astype(jnp.bfloat16),
    )


def pull_back(received, back_table):
    inner_width = HEADS * HEAD_DIM
    spread = HEADS * WIN * WIN
    flat = received.reshape(-1, received.shape[-1])
    query_heads = flat[:, :inner_width].reshape(-1, HEADS, HEAD_DIM)
    grad_heads = flat[:, inner_width : 2 * inner_width].reshape(-1, HEADS, HEAD_DIM)
    prob_piece = flat[:, 2 * inner_width : 2 * inner_width + spread].reshape(-1, HEADS, WIN * WIN)
    score_piece = flat[:, 2 * inner_width + spread :].reshape(-1, HEADS, WIN * WIN)
    score_dense = jnp.einsum(
        "qho,qok->hqk", score_piece, back_table, preferred_element_type=jnp.float32
    ).astype(jnp.bfloat16)
    prob_dense = jnp.einsum(
        "qho,qok->hqk", prob_piece, back_table, preferred_element_type=jnp.float32
    ).astype(jnp.bfloat16)
    grad_keys = jnp.einsum(
        "hqk,qhd->khd", score_dense, query_heads, preferred_element_type=jnp.float32
    )
    grad_values = jnp.einsum(
        "hqk,qhd->khd", prob_dense, grad_heads, preferred_element_type=jnp.float32
    )
    return (grad_keys * HEAD_DIM ** (-0.5), grad_values)


def shards(inputs, input_weight, output_weight, norm_gain, position_bias, cotangent):
    radius = WIN // 2
    inner_width = HEADS * HEAD_DIM
    score_scale = HEAD_DIM ** (-0.5)
    tile_rows, tile_cols = (inputs.shape[0], inputs.shape[1])
    cells = tile_rows * tile_cols
    wide_rows = tile_rows + 2 * radius
    wide_cols = tile_cols + 2 * radius
    first_row = lax.axis_index("lat") * tile_rows - radius
    global_rows = first_row + jnp.arange(wide_rows, dtype=jnp.int32)
    valid_rows = (global_rows >= 0) & (global_rows < tile_rows * lax.axis_size("lat"))
    row_keep = valid_rows.astype(jnp.bfloat16)[:, None, None]
    key_valid = (valid_rows[:, None] & jnp.ones((1, wide_cols), jnp.bool_)).reshape(-1)
    forward_table = window_table(tile_rows, tile_cols, radius, wide_rows, wide_cols, 0)
    table_low = forward_table.astype(jnp.bfloat16)
    query_row = jnp.arange(cells, dtype=jnp.int32) // tile_cols
    query_col = jnp.arange(cells, dtype=jnp.int32) % tile_cols
    key_row = jnp.arange(wide_rows * wide_cols, dtype=jnp.int32) // wide_cols
    key_col = jnp.arange(wide_rows * wide_cols, dtype=jnp.int32) % wide_cols
    step_row = key_row[None, :] - query_row[:, None]
    step_col = key_col[None, :] - query_col[:, None]
    in_window = (step_row >= 0) & (step_row < WIN) & (step_col >= 0) & (step_col < WIN)
    allowed = in_window & key_valid[None, :]
    back_table = window_table(wide_rows, wide_cols, 0, tile_rows, tile_cols, radius).astype(
        jnp.bfloat16
    )
    stream = inputs
    stored = []
    for layer_idx in range(LAYERS):
        wide_input = stream.astype(jnp.float32)
        normed_wide, pullback = jax.vjp(layer_norm, wide_input, norm_gain[layer_idx])
        normed = normed_wide.astype(jnp.bfloat16)
        packed = jnp.einsum(
            "abd,de->abe", normed, input_weight[layer_idx], preferred_element_type=jnp.float32
        ).astype(jnp.bfloat16)
        queries = packed[..., :inner_width]
        key_value = packed[..., inner_width:]
        pair_wide = extended(key_value, (("lat", 0), ("lon", 1)), radius)
        keys_wide = pair_wide[..., :inner_width]
        values_wide = pair_wide[..., inner_width:]
        attention, probs_low, mixed = attend(
            queries, keys_wide, values_wide, position_bias[layer_idx], allowed
        )
        branch = jnp.einsum(
            "abi,id->abd", mixed, output_weight[layer_idx], preferred_element_type=jnp.float32
        )
        stored.append(
            (pullback, normed, queries, keys_wide, values_wide, attention, probs_low, mixed)
        )
        stream = (wide_input + branch).astype(jnp.bfloat16)
    upstream = cotangent
    packed_terms = [None] * LAYERS
    output_terms = [None] * LAYERS
    gain_terms = [None] * LAYERS
    bias_terms = [None] * LAYERS
    for layer_idx in reversed(range(LAYERS)):
        pullback, normed, queries, keys_wide, values_wide, attention, probs_low, mixed = stored[
            layer_idx
        ]
        output_term = jnp.einsum("abi,abd->id", mixed, upstream, preferred_element_type=jnp.float32)
        output_part = lon_sum(output_term)
        grad_mixed = jnp.einsum(
            "abd,id->abi", upstream, output_weight[layer_idx], preferred_element_type=jnp.float32
        ).astype(jnp.bfloat16)
        grad_heads = grad_mixed.reshape(cells, HEADS, HEAD_DIM)
        key_heads = keys_wide.reshape(-1, HEADS, HEAD_DIM)
        value_heads = values_wide.reshape(-1, HEADS, HEAD_DIM)
        grad_probs = jnp.einsum(
            "qhd,khd->hqk", grad_heads, value_heads, preferred_element_type=jnp.float32
        )
        row_delta = jnp.sum(attention * grad_probs, axis=-1, keepdims=True)
        grad_scores = attention * (grad_probs - row_delta)
        bias_terms[layer_idx] = offset_sums(grad_scores, tile_rows, tile_cols)
        scores_low = grad_scores.astype(jnp.bfloat16)
        grad_query = jnp.einsum(
            "hqk,khd->qhd", scores_low, key_heads, preferred_element_type=jnp.float32
        )
        probs_offset = jnp.einsum(
            "hqk,qok->qho", probs_low, table_low, preferred_element_type=jnp.float32
        ).astype(jnp.bfloat16)
        scores_offset = jnp.einsum(
            "hqk,qok->qho", scores_low, table_low, preferred_element_type=jnp.float32
        ).astype(jnp.bfloat16)
        outgoing = jnp.concatenate(
            [
                queries,
                grad_mixed,
                probs_offset.reshape(tile_rows, tile_cols, HEADS * WIN * WIN),
                scores_offset.reshape(tile_rows, tile_cols, HEADS * WIN * WIN),
            ],
            axis=-1,
        )
        received = extended(outgoing, (("lat", 0), ("lon", 1)), radius) * row_keep
        grad_keys, grad_values = pull_back(received, back_table)
        grad_packed = jnp.concatenate(
            [
                (grad_query * score_scale).reshape(tile_rows, tile_cols, inner_width),
                grad_keys.reshape(tile_rows, tile_cols, inner_width),
                grad_values.reshape(tile_rows, tile_cols, inner_width),
            ],
            axis=-1,
        ).astype(jnp.bfloat16)
        packed_term = jnp.einsum(
            "abd,abe->de", normed, grad_packed, preferred_element_type=jnp.float32
        )
        grad_normed = jnp.einsum(
            "abe,de->abd", grad_packed, input_weight[layer_idx], preferred_element_type=jnp.float32
        )
        grad_wide, gain_term = pullback(grad_normed)
        gain_terms[layer_idx] = gain_term
        upstream = (upstream.astype(jnp.float32) + grad_wide).astype(jnp.bfloat16)
        packed_part = lon_sum(packed_term)
        summed = doubling_sum(jnp.concatenate([output_part, packed_part]), "lat", jnp.bfloat16)
        out_size = output_part.shape[0]
        output_terms[layer_idx] = summed[:out_size].reshape(-1, output_term.shape[1])
        packed_terms[layer_idx] = summed[out_size:].reshape(-1, packed_term.shape[1])
    stats = jnp.concatenate(
        [jnp.stack(gain_terms).reshape(-1), jnp.stack(bias_terms).reshape(-1)]
    )
    stats = doubling_sum(doubling_sum(stats, "lon", jnp.float32), "lat", jnp.float32)
    gain_count = LAYERS * norm_gain.shape[-1]
    gain_grad = stats[:gain_count].reshape(norm_gain.shape)
    bias_grad = stats[gain_count:].reshape(position_bias.shape)
    packed_grad = jnp.stack(packed_terms)
    output_grad = jnp.stack(output_terms)
    return (stream, upstream, packed_grad, output_grad, gain_grad, bias_grad)


def solution(mesh):
    return jax.shard_map(
        shards,
        mesh=mesh,
        in_specs=(P("lat", "lon", None), P(), P(), P(), P(), P("lat", "lon", None)),
        out_specs=(
            P("lat", "lon", None),
            P("lat", "lon", None),
            P(None, "lon", None),
            P(None, "lon", None),
            P(),
            P(),
        ),
        check_vma=False,
    )
```

```python
import jax
import jax.numpy as jnp
from jax import lax
from jax.sharding import PartitionSpec as P

HEADS = 8
HEAD_DIM = 64
WIN = 7
LAYERS = 2


eps = 1e-05


def extended(block, sides, width):
    for axis, dim in sides:
        count = lax.axis_size(axis)
        forward = [(i, i + 1) for i in range(count - 1)]
        forward.append((count - 1, 0))
        backward = [(target, source) for source, target in forward]
        low = lax.ppermute(
            lax.slice_in_dim(block, block.shape[dim] - width, None, axis=dim), axis, forward
        )
        high = lax.ppermute(lax.slice_in_dim(block, 0, width, axis=dim), axis, backward)
        block = jnp.concatenate([low, block, high], axis=dim)
    return block


def lon_sum(rows, extra=None):
    part = lax.psum_scatter(rows.astype(jnp.bfloat16), "lon", scatter_dimension=0, tiled=True)
    return part.reshape(-1)


def doubling_sum(value, axis, keep):
    count = lax.axis_size(axis)
    step = 1
    total = value
    while step < count:
        pairs = [(i, i ^ step) for i in range(count)]
        other = lax.ppermute(total, axis, pairs)
        total = total.astype(jnp.float32) + other.astype(jnp.float32)
        step *= 2
        if step < count:
            total = total.astype(keep)
    return total


def layer_norm(wide_input, gain):
    row_mean = jnp.mean(wide_input, axis=-1, keepdims=True)
    centred = wide_input - row_mean
    variance = jnp.mean(centred * centred, axis=-1, keepdims=True)
    return centred * lax.rsqrt(variance + eps) * gain


def cell_coords(rows, cols, shift):
    row_ids = jnp.arange(rows, dtype=jnp.int32)[:, None] + jnp.zeros((1, cols), jnp.int32) + shift
    col_ids = jnp.arange(cols, dtype=jnp.int32)[None, :] + jnp.zeros((rows, 1), jnp.int32) + shift
    return (row_ids.reshape(-1), col_ids.reshape(-1))


def window_table(query_rows, query_cols, query_shift, key_rows, key_cols, key_shift):
    radius = WIN // 2
    query_i, query_j = cell_coords(query_rows, query_cols, query_shift)
    key_i, key_j = cell_coords(key_rows, key_cols, key_shift)
    offsets = jnp.arange(WIN * WIN, dtype=jnp.int32)
    step_lat = offsets // WIN - radius
    step_lon = offsets % WIN - radius
    match_lat = key_i[None, None, :] - query_i[:, None, None] == step_lat[None, :, None]
    match_lon = key_j[None, None, :] - query_j[:, None, None] == step_lon[None, :, None]
    return match_lat & match_lon


def attend(queries, keys_wide, values_wide, bias, allowed, table_full):
    tile_rows, tile_cols = (queries.shape[0], queries.shape[1])
    score_scale = HEAD_DIM ** (-0.5)
    cells = tile_rows * tile_cols
    query_heads = queries.reshape(cells, HEADS, HEAD_DIM)
    key_heads = keys_wide.reshape(-1, HEADS, HEAD_DIM)
    value_heads = values_wide.reshape(-1, HEADS, HEAD_DIM)
    raw = jnp.einsum("qhd,khd->hqk", query_heads, key_heads, preferred_element_type=jnp.float32)
    bias_dense = jnp.einsum("ho,qok->hqk", bias, table_full, precision=lax.Precision.HIGHEST)
    scores = raw * score_scale + bias_dense
    masked = jnp.where(allowed[None], scores, -jnp.inf)
    row_max = jnp.max(masked, axis=-1, keepdims=True)
    weights_exp = jnp.exp(masked - row_max)
    attention = weights_exp / jnp.sum(weights_exp, axis=-1, keepdims=True)
    probs_low = attention.astype(jnp.bfloat16)
    mixed = jnp.einsum("hqk,khd->qhd", probs_low, value_heads, preferred_element_type=jnp.float32)
    return (
        attention,
        probs_low,
        mixed.reshape(tile_rows, tile_cols, HEADS * HEAD_DIM).astype(jnp.bfloat16),
    )


def pull_back(received, back_table):
    inner_width = HEADS * HEAD_DIM
    spread = HEADS * WIN * WIN
    flat = received.reshape(-1, received.shape[-1])
    query_heads = flat[:, :inner_width].reshape(-1, HEADS, HEAD_DIM)
    grad_heads = flat[:, inner_width : 2 * inner_width].reshape(-1, HEADS, HEAD_DIM)
    prob_piece = flat[:, 2 * inner_width : 2 * inner_width + spread].reshape(-1, HEADS, WIN * WIN)
    score_piece = flat[:, 2 * inner_width + spread :].reshape(-1, HEADS, WIN * WIN)
    score_dense = jnp.einsum(
        "qho,qok->hqk", score_piece, back_table, preferred_element_type=jnp.float32
    ).astype(jnp.bfloat16)
    prob_dense = jnp.einsum(
        "qho,qok->hqk", prob_piece, back_table, preferred_element_type=jnp.float32
    ).astype(jnp.bfloat16)
    grad_keys = jnp.einsum(
        "hqk,qhd->khd", score_dense, query_heads, preferred_element_type=jnp.float32
    )
    grad_values = jnp.einsum(
        "hqk,qhd->khd", prob_dense, grad_heads, preferred_element_type=jnp.float32
    )
    return (grad_keys * HEAD_DIM ** (-0.5), grad_values)


def shards(inputs, input_weight, output_weight, norm_gain, position_bias, cotangent):
    radius = WIN // 2
    inner_width = HEADS * HEAD_DIM
    score_scale = HEAD_DIM ** (-0.5)
    tile_rows, tile_cols = (inputs.shape[0], inputs.shape[1])
    cells = tile_rows * tile_cols
    wide_rows = tile_rows + 2 * radius
    wide_cols = tile_cols + 2 * radius
    first_row = lax.axis_index("lat") * tile_rows - radius
    global_rows = first_row + jnp.arange(wide_rows, dtype=jnp.int32)
    valid_rows = (global_rows >= 0) & (global_rows < tile_rows * lax.axis_size("lat"))
    row_keep = valid_rows.astype(jnp.bfloat16)[:, None, None]
    key_valid = (valid_rows[:, None] & jnp.ones((1, wide_cols), jnp.bool_)).reshape(-1)
    forward_table = window_table(tile_rows, tile_cols, radius, wide_rows, wide_cols, 0)
    table_low = forward_table.astype(jnp.bfloat16)
    table_full = forward_table.astype(jnp.float32)
    query_row = jnp.arange(cells, dtype=jnp.int32) // tile_cols
    query_col = jnp.arange(cells, dtype=jnp.int32) % tile_cols
    key_row = jnp.arange(wide_rows * wide_cols, dtype=jnp.int32) // wide_cols
    key_col = jnp.arange(wide_rows * wide_cols, dtype=jnp.int32) % wide_cols
    step_row = key_row[None, :] - query_row[:, None]
    step_col = key_col[None, :] - query_col[:, None]
    in_window = (step_row >= 0) & (step_row < WIN) & (step_col >= 0) & (step_col < WIN)
    allowed = in_window & key_valid[None, :]
    back_table = window_table(wide_rows, wide_cols, 0, tile_rows, tile_cols, radius).astype(
        jnp.bfloat16
    )
    stream = inputs
    stored = []
    for layer_idx in range(LAYERS):
        wide_input = stream.astype(jnp.float32)
        normed_wide, pullback = jax.vjp(layer_norm, wide_input, norm_gain[layer_idx])
        normed = normed_wide.astype(jnp.bfloat16)
        packed = jnp.einsum(
            "abd,de->abe", normed, input_weight[layer_idx], preferred_element_type=jnp.float32
        ).astype(jnp.bfloat16)
        queries = packed[..., :inner_width]
        key_value = packed[..., inner_width:]
        pair_wide = extended(key_value, (("lat", 0), ("lon", 1)), radius)
        keys_wide = pair_wide[..., :inner_width]
        values_wide = pair_wide[..., inner_width:]
        attention, probs_low, mixed = attend(
            queries, keys_wide, values_wide, position_bias[layer_idx], allowed, table_full
        )
        branch = jnp.einsum(
            "abi,id->abd", mixed, output_weight[layer_idx], preferred_element_type=jnp.float32
        )
        stored.append(
            (pullback, normed, queries, keys_wide, values_wide, attention, probs_low, mixed)
        )
        stream = (wide_input + branch).astype(jnp.bfloat16)
    upstream = cotangent
    packed_terms = [None] * LAYERS
    output_terms = [None] * LAYERS
    gain_terms = [None] * LAYERS
    bias_terms = [None] * LAYERS
    for layer_idx in reversed(range(LAYERS)):
        pullback, normed, queries, keys_wide, values_wide, attention, probs_low, mixed = stored[
            layer_idx
        ]
        output_term = jnp.einsum("abi,abd->id", mixed, upstream, preferred_element_type=jnp.float32)
        output_part = lon_sum(output_term)
        grad_mixed = jnp.einsum(
            "abd,id->abi", upstream, output_weight[layer_idx], preferred_element_type=jnp.float32
        ).astype(jnp.bfloat16)
        grad_heads = grad_mixed.reshape(cells, HEADS, HEAD_DIM)
        key_heads = keys_wide.reshape(-1, HEADS, HEAD_DIM)
        value_heads = values_wide.reshape(-1, HEADS, HEAD_DIM)
        grad_probs = jnp.einsum(
            "qhd,khd->hqk", grad_heads, value_heads, preferred_element_type=jnp.float32
        )
        row_delta = jnp.sum(attention * grad_probs, axis=-1, keepdims=True)
        grad_scores = attention * (grad_probs - row_delta)
        bias_terms[layer_idx] = jnp.einsum(
            "hqk,qok->ho", grad_scores, table_full, precision=lax.Precision.HIGHEST
        )
        scores_low = grad_scores.astype(jnp.bfloat16)
        grad_query = jnp.einsum(
            "hqk,khd->qhd", scores_low, key_heads, preferred_element_type=jnp.float32
        )
        probs_offset = jnp.einsum(
            "hqk,qok->qho", probs_low, table_low, preferred_element_type=jnp.float32
        ).astype(jnp.bfloat16)
        scores_offset = jnp.einsum(
            "hqk,qok->qho", scores_low, table_low, preferred_element_type=jnp.float32
        ).astype(jnp.bfloat16)
        outgoing = jnp.concatenate(
            [
                queries,
                grad_mixed,
                probs_offset.reshape(tile_rows, tile_cols, HEADS * WIN * WIN),
                scores_offset.reshape(tile_rows, tile_cols, HEADS * WIN * WIN),
            ],
            axis=-1,
        )
        received = extended(outgoing, (("lat", 0), ("lon", 1)), radius) * row_keep
        grad_keys, grad_values = pull_back(received, back_table)
        grad_packed = jnp.concatenate(
            [
                (grad_query * score_scale).reshape(tile_rows, tile_cols, inner_width),
                grad_keys.reshape(tile_rows, tile_cols, inner_width),
                grad_values.reshape(tile_rows, tile_cols, inner_width),
            ],
            axis=-1,
        ).astype(jnp.bfloat16)
        packed_term = jnp.einsum(
            "abd,abe->de", normed, grad_packed, preferred_element_type=jnp.float32
        )
        grad_normed = jnp.einsum(
            "abe,de->abd", grad_packed, input_weight[layer_idx], preferred_element_type=jnp.float32
        )
        grad_wide, gain_term = pullback(grad_normed)
        gain_terms[layer_idx] = gain_term
        upstream = (upstream.astype(jnp.float32) + grad_wide).astype(jnp.bfloat16)
        packed_part = lon_sum(packed_term)
        summed = doubling_sum(jnp.concatenate([output_part, packed_part]), "lat", jnp.bfloat16)
        out_size = output_part.shape[0]
        output_terms[layer_idx] = summed[:out_size].reshape(-1, output_term.shape[1])
        packed_terms[layer_idx] = summed[out_size:].reshape(-1, packed_term.shape[1])
    stats = jnp.concatenate(
        [jnp.stack(gain_terms).reshape(-1), jnp.stack(bias_terms).reshape(-1)]
    )
    stats = doubling_sum(doubling_sum(stats, "lon", jnp.float32), "lat", jnp.float32)
    gain_count = LAYERS * norm_gain.shape[-1]
    gain_grad = stats[:gain_count].reshape(norm_gain.shape)
    bias_grad = stats[gain_count:].reshape(position_bias.shape)
    packed_grad = jnp.stack(packed_terms)
    output_grad = jnp.stack(output_terms)
    return (stream, upstream, packed_grad, output_grad, gain_grad, bias_grad)


def solution(mesh):
    return jax.shard_map(
        shards,
        mesh=mesh,
        in_specs=(P("lat", "lon", None), P(), P(), P(), P(), P("lat", "lon", None)),
        out_specs=(
            P("lat", "lon", None),
            P("lat", "lon", None),
            P(None, "lon", None),
            P(None, "lon", None),
            P(),
            P(),
        ),
        check_vma=False,
    )
```

```python
import jax
import jax.numpy as jnp
from jax import lax
from jax.sharding import PartitionSpec as P

HEADS = 8
HEAD_DIM = 64
WIN = 7
LAYERS = 2


eps = 1e-05


def extended(block, sides, width):
    for axis, dim in sides:
        count = lax.axis_size(axis)
        forward = [(i, i + 1) for i in range(count - 1)]
        forward.append((count - 1, 0))
        backward = [(target, source) for source, target in forward]
        low = lax.ppermute(
            lax.slice_in_dim(block, block.shape[dim] - width, None, axis=dim), axis, forward
        )
        high = lax.ppermute(lax.slice_in_dim(block, 0, width, axis=dim), axis, backward)
        block = jnp.concatenate([low, block, high], axis=dim)
    return block


def lon_sum(rows, extra=None):
    part = lax.psum_scatter(rows.astype(jnp.bfloat16), "lon", scatter_dimension=0, tiled=True)
    return part.reshape(-1)


def exchange_sum(value, axis):
    count = lax.axis_size(axis)
    terms = [value.astype(jnp.float32)]
    for step in range(1, count):
        pairs = [(i, i ^ step) for i in range(count)]
        terms.append(lax.ppermute(value, axis, pairs).astype(jnp.float32))
    while len(terms) > 1:
        terms = [terms[k] + terms[k + 1] for k in range(0, len(terms), 2)]
    return terms[0]


def doubling_sum(value, axis, keep):
    count = lax.axis_size(axis)
    step = 1
    total = value
    while step < count:
        pairs = [(i, i ^ step) for i in range(count)]
        other = lax.ppermute(total, axis, pairs)
        total = total.astype(jnp.float32) + other.astype(jnp.float32)
        step *= 2
        if step < count:
            total = total.astype(keep)
    return total


def layer_norm(wide_input, gain):
    row_mean = jnp.mean(wide_input, axis=-1, keepdims=True)
    centred = wide_input - row_mean
    variance = jnp.mean(centred * centred, axis=-1, keepdims=True)
    return centred * lax.rsqrt(variance + eps) * gain


def cell_coords(rows, cols, shift):
    row_ids = jnp.arange(rows, dtype=jnp.int32)[:, None] + jnp.zeros((1, cols), jnp.int32) + shift
    col_ids = jnp.arange(cols, dtype=jnp.int32)[None, :] + jnp.zeros((rows, 1), jnp.int32) + shift
    return (row_ids.reshape(-1), col_ids.reshape(-1))


def window_table(query_rows, query_cols, query_shift, key_rows, key_cols, key_shift):
    radius = WIN // 2
    query_i, query_j = cell_coords(query_rows, query_cols, query_shift)
    key_i, key_j = cell_coords(key_rows, key_cols, key_shift)
    offsets = jnp.arange(WIN * WIN, dtype=jnp.int32)
    step_lat = offsets // WIN - radius
    step_lon = offsets % WIN - radius
    match_lat = key_i[None, None, :] - query_i[:, None, None] == step_lat[None, :, None]
    match_lon = key_j[None, None, :] - query_j[:, None, None] == step_lon[None, :, None]
    return match_lat & match_lon


def attend(queries, keys_wide, values_wide, bias, allowed, table_full):
    tile_rows, tile_cols = (queries.shape[0], queries.shape[1])
    score_scale = HEAD_DIM ** (-0.5)
    cells = tile_rows * tile_cols
    query_heads = queries.reshape(cells, HEADS, HEAD_DIM)
    key_heads = keys_wide.reshape(-1, HEADS, HEAD_DIM)
    value_heads = values_wide.reshape(-1, HEADS, HEAD_DIM)
    raw = jnp.einsum("qhd,khd->hqk", query_heads, key_heads, preferred_element_type=jnp.float32)
    bias_dense = jnp.einsum("ho,qok->hqk", bias, table_full, precision=lax.Precision.HIGHEST)
    scores = raw * score_scale + bias_dense
    masked = jnp.where(allowed[None], scores, -jnp.inf)
    row_max = jnp.max(masked, axis=-1, keepdims=True)
    weights_exp = jnp.exp(masked - row_max)
    attention = weights_exp / jnp.sum(weights_exp, axis=-1, keepdims=True)
    probs_low = attention.astype(jnp.bfloat16)
    mixed = jnp.einsum("hqk,khd->qhd", probs_low, value_heads, preferred_element_type=jnp.float32)
    return (
        attention,
        probs_low,
        mixed.reshape(tile_rows, tile_cols, HEADS * HEAD_DIM).astype(jnp.bfloat16),
    )


def pull_back(received, back_table):
    inner_width = HEADS * HEAD_DIM
    spread = HEADS * WIN * WIN
    flat = received.reshape(-1, received.shape[-1])
    query_heads = flat[:, :inner_width].reshape(-1, HEADS, HEAD_DIM)
    grad_heads = flat[:, inner_width : 2 * inner_width].reshape(-1, HEADS, HEAD_DIM)
    prob_piece = flat[:, 2 * inner_width : 2 * inner_width + spread].reshape(-1, HEADS, WIN * WIN)
    score_piece = flat[:, 2 * inner_width + spread :].reshape(-1, HEADS, WIN * WIN)
    score_dense = jnp.einsum(
        "qho,qok->hqk", score_piece, back_table, preferred_element_type=jnp.float32
    ).astype(jnp.bfloat16)
    prob_dense = jnp.einsum(
        "qho,qok->hqk", prob_piece, back_table, preferred_element_type=jnp.float32
    ).astype(jnp.bfloat16)
    grad_keys = jnp.einsum(
        "hqk,qhd->khd", score_dense, query_heads, preferred_element_type=jnp.float32
    )
    grad_values = jnp.einsum(
        "hqk,qhd->khd", prob_dense, grad_heads, preferred_element_type=jnp.float32
    )
    return (grad_keys * HEAD_DIM ** (-0.5), grad_values)


def shards(inputs, input_weight, output_weight, norm_gain, position_bias, cotangent):
    radius = WIN // 2
    inner_width = HEADS * HEAD_DIM
    score_scale = HEAD_DIM ** (-0.5)
    tile_rows, tile_cols = (inputs.shape[0], inputs.shape[1])
    cells = tile_rows * tile_cols
    wide_rows = tile_rows + 2 * radius
    wide_cols = tile_cols + 2 * radius
    first_row = lax.axis_index("lat") * tile_rows - radius
    global_rows = first_row + jnp.arange(wide_rows, dtype=jnp.int32)
    valid_rows = (global_rows >= 0) & (global_rows < tile_rows * lax.axis_size("lat"))
    row_keep = valid_rows.astype(jnp.bfloat16)[:, None, None]
    key_valid = (valid_rows[:, None] & jnp.ones((1, wide_cols), jnp.bool_)).reshape(-1)
    forward_table = window_table(tile_rows, tile_cols, radius, wide_rows, wide_cols, 0)
    table_low = forward_table.astype(jnp.bfloat16)
    table_full = forward_table.astype(jnp.float32)
    query_row = jnp.arange(cells, dtype=jnp.int32) // tile_cols
    query_col = jnp.arange(cells, dtype=jnp.int32) % tile_cols
    key_row = jnp.arange(wide_rows * wide_cols, dtype=jnp.int32) // wide_cols
    key_col = jnp.arange(wide_rows * wide_cols, dtype=jnp.int32) % wide_cols
    step_row = key_row[None, :] - query_row[:, None]
    step_col = key_col[None, :] - query_col[:, None]
    in_window = (step_row >= 0) & (step_row < WIN) & (step_col >= 0) & (step_col < WIN)
    allowed = in_window & key_valid[None, :]
    back_table = window_table(wide_rows, wide_cols, 0, tile_rows, tile_cols, radius).astype(
        jnp.bfloat16
    )
    stream = inputs
    stored = []
    for layer_idx in range(LAYERS):
        wide_input = stream.astype(jnp.float32)
        normed_wide, pullback = jax.vjp(layer_norm, wide_input, norm_gain[layer_idx])
        normed = normed_wide.astype(jnp.bfloat16)
        packed = jnp.einsum(
            "abd,de->abe", normed, input_weight[layer_idx], preferred_element_type=jnp.float32
        ).astype(jnp.bfloat16)
        queries = packed[..., :inner_width]
        key_value = packed[..., inner_width:]
        pair_wide = extended(key_value, (("lat", 0), ("lon", 1)), radius)
        keys_wide = pair_wide[..., :inner_width]
        values_wide = pair_wide[..., inner_width:]
        attention, probs_low, mixed = attend(
            queries, keys_wide, values_wide, position_bias[layer_idx], allowed, table_full
        )
        branch = jnp.einsum(
            "abi,id->abd", mixed, output_weight[layer_idx], preferred_element_type=jnp.float32
        )
        stored.append(
            (pullback, normed, queries, keys_wide, values_wide, attention, probs_low, mixed)
        )
        stream = (wide_input + branch).astype(jnp.bfloat16)
    upstream = cotangent
    packed_terms = [None] * LAYERS
    output_terms = [None] * LAYERS
    gain_terms = [None] * LAYERS
    bias_terms = [None] * LAYERS
    for layer_idx in reversed(range(LAYERS)):
        pullback, normed, queries, keys_wide, values_wide, attention, probs_low, mixed = stored[
            layer_idx
        ]
        output_term = jnp.einsum("abi,abd->id", mixed, upstream, preferred_element_type=jnp.float32)
        output_part = lon_sum(output_term)
        grad_mixed = jnp.einsum(
            "abd,id->abi", upstream, output_weight[layer_idx], preferred_element_type=jnp.float32
        ).astype(jnp.bfloat16)
        grad_heads = grad_mixed.reshape(cells, HEADS, HEAD_DIM)
        key_heads = keys_wide.reshape(-1, HEADS, HEAD_DIM)
        value_heads = values_wide.reshape(-1, HEADS, HEAD_DIM)
        grad_probs = jnp.einsum(
            "qhd,khd->hqk", grad_heads, value_heads, preferred_element_type=jnp.float32
        )
        row_delta = jnp.sum(attention * grad_probs, axis=-1, keepdims=True)
        grad_scores = attention * (grad_probs - row_delta)
        bias_terms[layer_idx] = jnp.einsum(
            "hqk,qok->ho", grad_scores, table_full, precision=lax.Precision.HIGHEST
        )
        scores_low = grad_scores.astype(jnp.bfloat16)
        grad_query = jnp.einsum(
            "hqk,khd->qhd", scores_low, key_heads, preferred_element_type=jnp.float32
        )
        probs_offset = jnp.einsum(
            "hqk,qok->qho", probs_low, table_low, preferred_element_type=jnp.float32
        ).astype(jnp.bfloat16)
        scores_offset = jnp.einsum(
            "hqk,qok->qho", scores_low, table_low, preferred_element_type=jnp.float32
        ).astype(jnp.bfloat16)
        outgoing = jnp.concatenate(
            [
                queries,
                grad_mixed,
                probs_offset.reshape(tile_rows, tile_cols, HEADS * WIN * WIN),
                scores_offset.reshape(tile_rows, tile_cols, HEADS * WIN * WIN),
            ],
            axis=-1,
        )
        received = extended(outgoing, (("lat", 0), ("lon", 1)), radius) * row_keep
        grad_keys, grad_values = pull_back(received, back_table)
        grad_packed = jnp.concatenate(
            [
                (grad_query * score_scale).reshape(tile_rows, tile_cols, inner_width),
                grad_keys.reshape(tile_rows, tile_cols, inner_width),
                grad_values.reshape(tile_rows, tile_cols, inner_width),
            ],
            axis=-1,
        ).astype(jnp.bfloat16)
        packed_term = jnp.einsum(
            "abd,abe->de", normed, grad_packed, preferred_element_type=jnp.float32
        )
        grad_normed = jnp.einsum(
            "abe,de->abd", grad_packed, input_weight[layer_idx], preferred_element_type=jnp.float32
        )
        grad_wide, gain_term = pullback(grad_normed)
        gain_terms[layer_idx] = gain_term
        upstream = (upstream.astype(jnp.float32) + grad_wide).astype(jnp.bfloat16)
        packed_part = lon_sum(packed_term)
        output_terms[layer_idx] = exchange_sum(output_part, "lat").reshape(-1, output_term.shape[1])
        packed_terms[layer_idx] = exchange_sum(packed_part, "lat").reshape(-1, packed_term.shape[1])
    stats = jnp.concatenate(
        [jnp.stack(gain_terms).reshape(-1), jnp.stack(bias_terms).reshape(-1)]
    )
    stats = doubling_sum(doubling_sum(stats, "lon", jnp.float32), "lat", jnp.float32)
    gain_count = LAYERS * norm_gain.shape[-1]
    gain_grad = stats[:gain_count].reshape(norm_gain.shape)
    bias_grad = stats[gain_count:].reshape(position_bias.shape)
    packed_grad = jnp.stack(packed_terms)
    output_grad = jnp.stack(output_terms)
    return (stream, upstream, packed_grad, output_grad, gain_grad, bias_grad)


def solution(mesh):
    return jax.shard_map(
        shards,
        mesh=mesh,
        in_specs=(P("lat", "lon", None), P(), P(), P(), P(), P("lat", "lon", None)),
        out_specs=(
            P("lat", "lon", None),
            P("lat", "lon", None),
            P(None, "lon", None),
            P(None, "lon", None),
            P(),
            P(),
        ),
        check_vma=False,
    )
```

```python
import jax
import jax.numpy as jnp
from jax import lax
from jax.sharding import PartitionSpec as P

HEADS = 8
HEAD_DIM = 64
WIN = 7
LAYERS = 2


eps = 1e-05


def extended(block, sides, width):
    for axis, dim in sides:
        count = lax.axis_size(axis)
        forward = [(i, i + 1) for i in range(count - 1)]
        forward.append((count - 1, 0))
        backward = [(target, source) for source, target in forward]
        low = lax.ppermute(
            lax.slice_in_dim(block, block.shape[dim] - width, None, axis=dim), axis, forward
        )
        high = lax.ppermute(lax.slice_in_dim(block, 0, width, axis=dim), axis, backward)
        block = jnp.concatenate([low, block, high], axis=dim)
    return block


def lon_sum(rows, extra=None):
    count = lax.axis_size("lon")
    me = lax.axis_index("lon")
    held = rows.astype(jnp.float32).reshape((count, -1) + rows.shape[1:])
    step = 1
    while step < count:
        split = held.reshape((held.shape[0] // 2, 2) + held.shape[1:])
        upper = (me // step) % 2 == 1
        keep = jnp.where(upper, split[:, 1], split[:, 0])
        send = jnp.where(upper, split[:, 0], split[:, 1]).astype(jnp.bfloat16)
        pairs = [(i, i ^ step) for i in range(count)]
        held = keep + lax.ppermute(send, "lon", pairs).astype(jnp.float32)
        step *= 2
    return held.astype(jnp.bfloat16).reshape(-1)


def doubling_sum(value, axis, keep):
    count = lax.axis_size(axis)
    step = 1
    total = value
    while step < count:
        pairs = [(i, i ^ step) for i in range(count)]
        other = lax.ppermute(total, axis, pairs)
        total = total.astype(jnp.float32) + other.astype(jnp.float32)
        step *= 2
        if step < count:
            total = total.astype(keep)
    return total


def layer_norm(wide_input, gain):
    row_mean = jnp.mean(wide_input, axis=-1, keepdims=True)
    centred = wide_input - row_mean
    variance = jnp.mean(centred * centred, axis=-1, keepdims=True)
    return centred * lax.rsqrt(variance + eps) * gain


def cell_coords(rows, cols, shift):
    row_ids = jnp.arange(rows, dtype=jnp.int32)[:, None] + jnp.zeros((1, cols), jnp.int32) + shift
    col_ids = jnp.arange(cols, dtype=jnp.int32)[None, :] + jnp.zeros((rows, 1), jnp.int32) + shift
    return (row_ids.reshape(-1), col_ids.reshape(-1))


def window_table(query_rows, query_cols, query_shift, key_rows, key_cols, key_shift):
    radius = WIN // 2
    query_i, query_j = cell_coords(query_rows, query_cols, query_shift)
    key_i, key_j = cell_coords(key_rows, key_cols, key_shift)
    offsets = jnp.arange(WIN * WIN, dtype=jnp.int32)
    step_lat = offsets // WIN - radius
    step_lon = offsets % WIN - radius
    match_lat = key_i[None, None, :] - query_i[:, None, None] == step_lat[None, :, None]
    match_lon = key_j[None, None, :] - query_j[:, None, None] == step_lon[None, :, None]
    return match_lat & match_lon


def attend(queries, keys_wide, values_wide, bias, allowed, table_full):
    tile_rows, tile_cols = (queries.shape[0], queries.shape[1])
    score_scale = HEAD_DIM ** (-0.5)
    cells = tile_rows * tile_cols
    query_heads = queries.reshape(cells, HEADS, HEAD_DIM)
    key_heads = keys_wide.reshape(-1, HEADS, HEAD_DIM)
    value_heads = values_wide.reshape(-1, HEADS, HEAD_DIM)
    raw = jnp.einsum("qhd,khd->hqk", query_heads, key_heads, preferred_element_type=jnp.float32)
    bias_dense = jnp.einsum("ho,qok->hqk", bias, table_full, precision=lax.Precision.HIGHEST)
    scores = raw * score_scale + bias_dense
    masked = jnp.where(allowed[None], scores, -jnp.inf)
    row_max = jnp.max(masked, axis=-1, keepdims=True)
    weights_exp = jnp.exp(masked - row_max)
    attention = weights_exp / jnp.sum(weights_exp, axis=-1, keepdims=True)
    probs_low = attention.astype(jnp.bfloat16)
    mixed = jnp.einsum("hqk,khd->qhd", probs_low, value_heads, preferred_element_type=jnp.float32)
    return (
        attention,
        probs_low,
        mixed.reshape(tile_rows, tile_cols, HEADS * HEAD_DIM).astype(jnp.bfloat16),
    )


def pull_back(received, back_table):
    inner_width = HEADS * HEAD_DIM
    spread = HEADS * WIN * WIN
    flat = received.reshape(-1, received.shape[-1])
    query_heads = flat[:, :inner_width].reshape(-1, HEADS, HEAD_DIM)
    grad_heads = flat[:, inner_width : 2 * inner_width].reshape(-1, HEADS, HEAD_DIM)
    prob_piece = flat[:, 2 * inner_width : 2 * inner_width + spread].reshape(-1, HEADS, WIN * WIN)
    score_piece = flat[:, 2 * inner_width + spread :].reshape(-1, HEADS, WIN * WIN)
    score_dense = jnp.einsum(
        "qho,qok->hqk", score_piece, back_table, preferred_element_type=jnp.float32
    ).astype(jnp.bfloat16)
    prob_dense = jnp.einsum(
        "qho,qok->hqk", prob_piece, back_table, preferred_element_type=jnp.float32
    ).astype(jnp.bfloat16)
    grad_keys = jnp.einsum(
        "hqk,qhd->khd", score_dense, query_heads, preferred_element_type=jnp.float32
    )
    grad_values = jnp.einsum(
        "hqk,qhd->khd", prob_dense, grad_heads, preferred_element_type=jnp.float32
    )
    return (grad_keys * HEAD_DIM ** (-0.5), grad_values)


def shards(inputs, input_weight, output_weight, norm_gain, position_bias, cotangent):
    radius = WIN // 2
    inner_width = HEADS * HEAD_DIM
    score_scale = HEAD_DIM ** (-0.5)
    tile_rows, tile_cols = (inputs.shape[0], inputs.shape[1])
    cells = tile_rows * tile_cols
    wide_rows = tile_rows + 2 * radius
    wide_cols = tile_cols + 2 * radius
    first_row = lax.axis_index("lat") * tile_rows - radius
    global_rows = first_row + jnp.arange(wide_rows, dtype=jnp.int32)
    valid_rows = (global_rows >= 0) & (global_rows < tile_rows * lax.axis_size("lat"))
    row_keep = valid_rows.astype(jnp.bfloat16)[:, None, None]
    key_valid = (valid_rows[:, None] & jnp.ones((1, wide_cols), jnp.bool_)).reshape(-1)
    forward_table = window_table(tile_rows, tile_cols, radius, wide_rows, wide_cols, 0)
    table_low = forward_table.astype(jnp.bfloat16)
    table_full = forward_table.astype(jnp.float32)
    query_row = jnp.arange(cells, dtype=jnp.int32) // tile_cols
    query_col = jnp.arange(cells, dtype=jnp.int32) % tile_cols
    key_row = jnp.arange(wide_rows * wide_cols, dtype=jnp.int32) // wide_cols
    key_col = jnp.arange(wide_rows * wide_cols, dtype=jnp.int32) % wide_cols
    step_row = key_row[None, :] - query_row[:, None]
    step_col = key_col[None, :] - query_col[:, None]
    in_window = (step_row >= 0) & (step_row < WIN) & (step_col >= 0) & (step_col < WIN)
    allowed = in_window & key_valid[None, :]
    back_table = window_table(wide_rows, wide_cols, 0, tile_rows, tile_cols, radius).astype(
        jnp.bfloat16
    )
    stream = inputs
    stored = []
    for layer_idx in range(LAYERS):
        wide_input = stream.astype(jnp.float32)
        normed_wide, pullback = jax.vjp(layer_norm, wide_input, norm_gain[layer_idx])
        normed = normed_wide.astype(jnp.bfloat16)
        packed = jnp.einsum(
            "abd,de->abe", normed, input_weight[layer_idx], preferred_element_type=jnp.float32
        ).astype(jnp.bfloat16)
        queries = packed[..., :inner_width]
        key_value = packed[..., inner_width:]
        pair_wide = extended(key_value, (("lat", 0), ("lon", 1)), radius)
        keys_wide = pair_wide[..., :inner_width]
        values_wide = pair_wide[..., inner_width:]
        attention, probs_low, mixed = attend(
            queries, keys_wide, values_wide, position_bias[layer_idx], allowed, table_full
        )
        branch = jnp.einsum(
            "abi,id->abd", mixed, output_weight[layer_idx], preferred_element_type=jnp.float32
        )
        stored.append(
            (pullback, normed, queries, keys_wide, values_wide, attention, probs_low, mixed)
        )
        stream = (wide_input + branch).astype(jnp.bfloat16)
    upstream = cotangent
    packed_terms = [None] * LAYERS
    output_terms = [None] * LAYERS
    gain_terms = [None] * LAYERS
    bias_terms = [None] * LAYERS
    for layer_idx in reversed(range(LAYERS)):
        pullback, normed, queries, keys_wide, values_wide, attention, probs_low, mixed = stored[
            layer_idx
        ]
        output_term = jnp.einsum("abi,abd->id", mixed, upstream, preferred_element_type=jnp.float32)
        output_part = lon_sum(output_term)
        grad_mixed = jnp.einsum(
            "abd,id->abi", upstream, output_weight[layer_idx], preferred_element_type=jnp.float32
        ).astype(jnp.bfloat16)
        grad_heads = grad_mixed.reshape(cells, HEADS, HEAD_DIM)
        key_heads = keys_wide.reshape(-1, HEADS, HEAD_DIM)
        value_heads = values_wide.reshape(-1, HEADS, HEAD_DIM)
        grad_probs = jnp.einsum(
            "qhd,khd->hqk", grad_heads, value_heads, preferred_element_type=jnp.float32
        )
        row_delta = jnp.sum(attention * grad_probs, axis=-1, keepdims=True)
        grad_scores = attention * (grad_probs - row_delta)
        bias_terms[layer_idx] = jnp.einsum(
            "hqk,qok->ho", grad_scores, table_full, precision=lax.Precision.HIGHEST
        )
        scores_low = grad_scores.astype(jnp.bfloat16)
        grad_query = jnp.einsum(
            "hqk,khd->qhd", scores_low, key_heads, preferred_element_type=jnp.float32
        )
        probs_offset = jnp.einsum(
            "hqk,qok->qho", probs_low, table_low, preferred_element_type=jnp.float32
        ).astype(jnp.bfloat16)
        scores_offset = jnp.einsum(
            "hqk,qok->qho", scores_low, table_low, preferred_element_type=jnp.float32
        ).astype(jnp.bfloat16)
        outgoing = jnp.concatenate(
            [
                queries,
                grad_mixed,
                probs_offset.reshape(tile_rows, tile_cols, HEADS * WIN * WIN),
                scores_offset.reshape(tile_rows, tile_cols, HEADS * WIN * WIN),
            ],
            axis=-1,
        )
        received = extended(outgoing, (("lat", 0), ("lon", 1)), radius) * row_keep
        grad_keys, grad_values = pull_back(received, back_table)
        grad_packed = jnp.concatenate(
            [
                (grad_query * score_scale).reshape(tile_rows, tile_cols, inner_width),
                grad_keys.reshape(tile_rows, tile_cols, inner_width),
                grad_values.reshape(tile_rows, tile_cols, inner_width),
            ],
            axis=-1,
        ).astype(jnp.bfloat16)
        packed_term = jnp.einsum(
            "abd,abe->de", normed, grad_packed, preferred_element_type=jnp.float32
        )
        grad_normed = jnp.einsum(
            "abe,de->abd", grad_packed, input_weight[layer_idx], preferred_element_type=jnp.float32
        )
        grad_wide, gain_term = pullback(grad_normed)
        gain_terms[layer_idx] = gain_term
        upstream = (upstream.astype(jnp.float32) + grad_wide).astype(jnp.bfloat16)
        packed_part = lon_sum(packed_term)
        summed = doubling_sum(jnp.concatenate([output_part, packed_part]), "lat", jnp.bfloat16)
        out_size = output_part.shape[0]
        output_terms[layer_idx] = summed[:out_size].reshape(-1, output_term.shape[1])
        packed_terms[layer_idx] = summed[out_size:].reshape(-1, packed_term.shape[1])
    stats = jnp.concatenate(
        [jnp.stack(gain_terms).reshape(-1), jnp.stack(bias_terms).reshape(-1)]
    )
    stats = doubling_sum(doubling_sum(stats, "lon", jnp.float32), "lat", jnp.float32)
    gain_count = LAYERS * norm_gain.shape[-1]
    gain_grad = stats[:gain_count].reshape(norm_gain.shape)
    bias_grad = stats[gain_count:].reshape(position_bias.shape)
    packed_grad = jnp.stack(packed_terms)
    output_grad = jnp.stack(output_terms)
    return (stream, upstream, packed_grad, output_grad, gain_grad, bias_grad)


def solution(mesh):
    return jax.shard_map(
        shards,
        mesh=mesh,
        in_specs=(P("lat", "lon", None), P(), P(), P(), P(), P("lat", "lon", None)),
        out_specs=(
            P("lat", "lon", None),
            P("lat", "lon", None),
            P(None, "lon", None),
            P(None, "lon", None),
            P(),
            P(),
        ),
        check_vma=False,
    )
```

```python
import jax
import jax.numpy as jnp
from jax import lax
from jax.sharding import PartitionSpec as P

HEADS = 8
HEAD_DIM = 64
WIN = 7
LAYERS = 2


eps = 1e-05


def extended(block, sides, width):
    for axis, dim in sides:
        count = lax.axis_size(axis)
        forward = [(i, i + 1) for i in range(count - 1)]
        forward.append((count - 1, 0))
        backward = [(target, source) for source, target in forward]
        low = lax.ppermute(
            lax.slice_in_dim(block, block.shape[dim] - width, None, axis=dim), axis, forward
        )
        high = lax.ppermute(lax.slice_in_dim(block, 0, width, axis=dim), axis, backward)
        block = jnp.concatenate([low, block, high], axis=dim)
    return block


def lon_sum(rows, extra=None):
    part = lax.psum_scatter(rows.astype(jnp.bfloat16), "lon", scatter_dimension=0, tiled=True)
    return part.reshape(-1)


def doubling_sum(value, axis, keep):
    count = lax.axis_size(axis)
    step = 1
    total = value
    while step < count:
        pairs = [(i, i ^ step) for i in range(count)]
        other = lax.ppermute(total, axis, pairs)
        total = total.astype(jnp.float32) + other.astype(jnp.float32)
        step *= 2
        if step < count:
            total = total.astype(keep)
    return total


def balanced_sum(value, axis, keep):
    count = lax.axis_size(axis)
    steps = []
    step = 1
    while step < count:
        steps.append(step)
        step *= 2
    half = value.shape[0] // 2
    totals = [value[:half], value[half:]]
    orders = [steps, steps[::-1]]
    for level in range(len(steps)):
        for k in range(2):
            pairs = [(i, i ^ orders[k][level]) for i in range(count)]
            other = lax.ppermute(totals[k], axis, pairs)
            totals[k] = totals[k].astype(jnp.float32) + other.astype(jnp.float32)
            if level + 1 < len(steps):
                totals[k] = totals[k].astype(keep)
    return jnp.concatenate(totals)


def layer_norm(wide_input, gain):
    row_mean = jnp.mean(wide_input, axis=-1, keepdims=True)
    centred = wide_input - row_mean
    variance = jnp.mean(centred * centred, axis=-1, keepdims=True)
    return centred * lax.rsqrt(variance + eps) * gain


def cell_coords(rows, cols, shift):
    row_ids = jnp.arange(rows, dtype=jnp.int32)[:, None] + jnp.zeros((1, cols), jnp.int32) + shift
    col_ids = jnp.arange(cols, dtype=jnp.int32)[None, :] + jnp.zeros((rows, 1), jnp.int32) + shift
    return (row_ids.reshape(-1), col_ids.reshape(-1))


def window_table(query_rows, query_cols, query_shift, key_rows, key_cols, key_shift):
    radius = WIN // 2
    query_i, query_j = cell_coords(query_rows, query_cols, query_shift)
    key_i, key_j = cell_coords(key_rows, key_cols, key_shift)
    offsets = jnp.arange(WIN * WIN, dtype=jnp.int32)
    step_lat = offsets // WIN - radius
    step_lon = offsets % WIN - radius
    match_lat = key_i[None, None, :] - query_i[:, None, None] == step_lat[None, :, None]
    match_lon = key_j[None, None, :] - query_j[:, None, None] == step_lon[None, :, None]
    return match_lat & match_lon


def attend(queries, keys_wide, values_wide, bias, allowed, table_full):
    tile_rows, tile_cols = (queries.shape[0], queries.shape[1])
    score_scale = HEAD_DIM ** (-0.5)
    cells = tile_rows * tile_cols
    query_heads = queries.reshape(cells, HEADS, HEAD_DIM)
    key_heads = keys_wide.reshape(-1, HEADS, HEAD_DIM)
    value_heads = values_wide.reshape(-1, HEADS, HEAD_DIM)
    raw = jnp.einsum("qhd,khd->hqk", query_heads, key_heads, preferred_element_type=jnp.float32)
    bias_dense = jnp.einsum("ho,qok->hqk", bias, table_full, precision=lax.Precision.HIGHEST)
    scores = raw * score_scale + bias_dense
    masked = jnp.where(allowed[None], scores, -jnp.inf)
    row_max = jnp.max(masked, axis=-1, keepdims=True)
    weights_exp = jnp.exp(masked - row_max)
    attention = weights_exp / jnp.sum(weights_exp, axis=-1, keepdims=True)
    probs_low = attention.astype(jnp.bfloat16)
    mixed = jnp.einsum("hqk,khd->qhd", probs_low, value_heads, preferred_element_type=jnp.float32)
    return (
        attention,
        probs_low,
        mixed.reshape(tile_rows, tile_cols, HEADS * HEAD_DIM).astype(jnp.bfloat16),
    )


def pull_back(received, back_table):
    inner_width = HEADS * HEAD_DIM
    spread = HEADS * WIN * WIN
    flat = received.reshape(-1, received.shape[-1])
    query_heads = flat[:, :inner_width].reshape(-1, HEADS, HEAD_DIM)
    grad_heads = flat[:, inner_width : 2 * inner_width].reshape(-1, HEADS, HEAD_DIM)
    prob_piece = flat[:, 2 * inner_width : 2 * inner_width + spread].reshape(-1, HEADS, WIN * WIN)
    score_piece = flat[:, 2 * inner_width + spread :].reshape(-1, HEADS, WIN * WIN)
    score_dense = jnp.einsum(
        "qho,qok->hqk", score_piece, back_table, preferred_element_type=jnp.float32
    ).astype(jnp.bfloat16)
    prob_dense = jnp.einsum(
        "qho,qok->hqk", prob_piece, back_table, preferred_element_type=jnp.float32
    ).astype(jnp.bfloat16)
    grad_keys = jnp.einsum(
        "hqk,qhd->khd", score_dense, query_heads, preferred_element_type=jnp.float32
    )
    grad_values = jnp.einsum(
        "hqk,qhd->khd", prob_dense, grad_heads, preferred_element_type=jnp.float32
    )
    return (grad_keys * HEAD_DIM ** (-0.5), grad_values)


def shards(inputs, input_weight, output_weight, norm_gain, position_bias, cotangent):
    radius = WIN // 2
    inner_width = HEADS * HEAD_DIM
    score_scale = HEAD_DIM ** (-0.5)
    tile_rows, tile_cols = (inputs.shape[0], inputs.shape[1])
    cells = tile_rows * tile_cols
    wide_rows = tile_rows + 2 * radius
    wide_cols = tile_cols + 2 * radius
    first_row = lax.axis_index("lat") * tile_rows - radius
    global_rows = first_row + jnp.arange(wide_rows, dtype=jnp.int32)
    valid_rows = (global_rows >= 0) & (global_rows < tile_rows * lax.axis_size("lat"))
    row_keep = valid_rows.astype(jnp.bfloat16)[:, None, None]
    key_valid = (valid_rows[:, None] & jnp.ones((1, wide_cols), jnp.bool_)).reshape(-1)
    forward_table = window_table(tile_rows, tile_cols, radius, wide_rows, wide_cols, 0)
    table_low = forward_table.astype(jnp.bfloat16)
    table_full = forward_table.astype(jnp.float32)
    query_row = jnp.arange(cells, dtype=jnp.int32) // tile_cols
    query_col = jnp.arange(cells, dtype=jnp.int32) % tile_cols
    key_row = jnp.arange(wide_rows * wide_cols, dtype=jnp.int32) // wide_cols
    key_col = jnp.arange(wide_rows * wide_cols, dtype=jnp.int32) % wide_cols
    step_row = key_row[None, :] - query_row[:, None]
    step_col = key_col[None, :] - query_col[:, None]
    in_window = (step_row >= 0) & (step_row < WIN) & (step_col >= 0) & (step_col < WIN)
    allowed = in_window & key_valid[None, :]
    back_table = window_table(wide_rows, wide_cols, 0, tile_rows, tile_cols, radius).astype(
        jnp.bfloat16
    )
    stream = inputs
    stored = []
    for layer_idx in range(LAYERS):
        wide_input = stream.astype(jnp.float32)
        normed_wide, pullback = jax.vjp(layer_norm, wide_input, norm_gain[layer_idx])
        normed = normed_wide.astype(jnp.bfloat16)
        packed = jnp.einsum(
            "abd,de->abe", normed, input_weight[layer_idx], preferred_element_type=jnp.float32
        ).astype(jnp.bfloat16)
        queries = packed[..., :inner_width]
        key_value = packed[..., inner_width:]
        pair_wide = extended(key_value, (("lat", 0), ("lon", 1)), radius)
        keys_wide = pair_wide[..., :inner_width]
        values_wide = pair_wide[..., inner_width:]
        attention, probs_low, mixed = attend(
            queries, keys_wide, values_wide, position_bias[layer_idx], allowed, table_full
        )
        branch = jnp.einsum(
            "abi,id->abd", mixed, output_weight[layer_idx], preferred_element_type=jnp.float32
        )
        stored.append(
            (pullback, normed, queries, keys_wide, values_wide, attention, probs_low, mixed)
        )
        stream = (wide_input + branch).astype(jnp.bfloat16)
    upstream = cotangent
    packed_terms = [None] * LAYERS
    output_terms = [None] * LAYERS
    gain_terms = [None] * LAYERS
    bias_terms = [None] * LAYERS
    for layer_idx in reversed(range(LAYERS)):
        pullback, normed, queries, keys_wide, values_wide, attention, probs_low, mixed = stored[
            layer_idx
        ]
        output_term = jnp.einsum("abi,abd->id", mixed, upstream, preferred_element_type=jnp.float32)
        output_part = lon_sum(output_term)
        grad_mixed = jnp.einsum(
            "abd,id->abi", upstream, output_weight[layer_idx], preferred_element_type=jnp.float32
        ).astype(jnp.bfloat16)
        grad_heads = grad_mixed.reshape(cells, HEADS, HEAD_DIM)
        key_heads = keys_wide.reshape(-1, HEADS, HEAD_DIM)
        value_heads = values_wide.reshape(-1, HEADS, HEAD_DIM)
        grad_probs = jnp.einsum(
            "qhd,khd->hqk", grad_heads, value_heads, preferred_element_type=jnp.float32
        )
        row_delta = jnp.sum(attention * grad_probs, axis=-1, keepdims=True)
        grad_scores = attention * (grad_probs - row_delta)
        bias_terms[layer_idx] = jnp.einsum(
            "hqk,qok->ho", grad_scores, table_full, precision=lax.Precision.HIGHEST
        )
        scores_low = grad_scores.astype(jnp.bfloat16)
        grad_query = jnp.einsum(
            "hqk,khd->qhd", scores_low, key_heads, preferred_element_type=jnp.float32
        )
        probs_offset = jnp.einsum(
            "hqk,qok->qho", probs_low, table_low, preferred_element_type=jnp.float32
        ).astype(jnp.bfloat16)
        scores_offset = jnp.einsum(
            "hqk,qok->qho", scores_low, table_low, preferred_element_type=jnp.float32
        ).astype(jnp.bfloat16)
        outgoing = jnp.concatenate(
            [
                queries,
                grad_mixed,
                probs_offset.reshape(tile_rows, tile_cols, HEADS * WIN * WIN),
                scores_offset.reshape(tile_rows, tile_cols, HEADS * WIN * WIN),
            ],
            axis=-1,
        )
        received = extended(outgoing, (("lat", 0), ("lon", 1)), radius) * row_keep
        grad_keys, grad_values = pull_back(received, back_table)
        grad_packed = jnp.concatenate(
            [
                (grad_query * score_scale).reshape(tile_rows, tile_cols, inner_width),
                grad_keys.reshape(tile_rows, tile_cols, inner_width),
                grad_values.reshape(tile_rows, tile_cols, inner_width),
            ],
            axis=-1,
        ).astype(jnp.bfloat16)
        packed_term = jnp.einsum(
            "abd,abe->de", normed, grad_packed, preferred_element_type=jnp.float32
        )
        grad_normed = jnp.einsum(
            "abe,de->abd", grad_packed, input_weight[layer_idx], preferred_element_type=jnp.float32
        )
        grad_wide, gain_term = pullback(grad_normed)
        gain_terms[layer_idx] = gain_term
        upstream = (upstream.astype(jnp.float32) + grad_wide).astype(jnp.bfloat16)
        packed_part = lon_sum(packed_term)
        summed = balanced_sum(jnp.concatenate([output_part, packed_part]), "lat", jnp.bfloat16)
        out_size = output_part.shape[0]
        output_terms[layer_idx] = summed[:out_size].reshape(-1, output_term.shape[1])
        packed_terms[layer_idx] = summed[out_size:].reshape(-1, packed_term.shape[1])
    stats = jnp.concatenate(
        [jnp.stack(gain_terms).reshape(-1), jnp.stack(bias_terms).reshape(-1)]
    )
    stats = doubling_sum(doubling_sum(stats, "lon", jnp.float32), "lat", jnp.float32)
    gain_count = LAYERS * norm_gain.shape[-1]
    gain_grad = stats[:gain_count].reshape(norm_gain.shape)
    bias_grad = stats[gain_count:].reshape(position_bias.shape)
    packed_grad = jnp.stack(packed_terms)
    output_grad = jnp.stack(output_terms)
    return (stream, upstream, packed_grad, output_grad, gain_grad, bias_grad)


def solution(mesh):
    return jax.shard_map(
        shards,
        mesh=mesh,
        in_specs=(P("lat", "lon", None), P(), P(), P(), P(), P("lat", "lon", None)),
        out_specs=(
            P("lat", "lon", None),
            P("lat", "lon", None),
            P(None, "lon", None),
            P(None, "lon", None),
            P(),
            P(),
        ),
        check_vma=False,
    )
```

```python
import jax
import jax.numpy as jnp
from jax import lax
from jax.sharding import PartitionSpec as P

HEADS = 8
HEAD_DIM = 64
WIN = 7
LAYERS = 2


eps = 1e-05


def extended(block, sides, width):
    for axis, dim in sides:
        count = lax.axis_size(axis)
        forward = [(i, i + 1) for i in range(count - 1)]
        forward.append((count - 1, 0))
        backward = [(target, source) for source, target in forward]
        low = lax.ppermute(
            lax.slice_in_dim(block, block.shape[dim] - width, None, axis=dim), axis, forward
        )
        high = lax.ppermute(lax.slice_in_dim(block, 0, width, axis=dim), axis, backward)
        block = jnp.concatenate([low, block, high], axis=dim)
    return block


def lon_sum(rows, extra=None):
    part = lax.psum_scatter(rows.astype(jnp.bfloat16), "lon", scatter_dimension=0, tiled=True)
    return part.reshape(-1)


def doubling_sum(value, axis, keep):
    count = lax.axis_size(axis)
    step = 1
    total = value
    while step < count:
        pairs = [(i, i ^ step) for i in range(count)]
        other = lax.ppermute(total, axis, pairs)
        total = total.astype(jnp.float32) + other.astype(jnp.float32)
        step *= 2
        if step < count:
            total = total.astype(keep)
    return total


def folded(block, sides, width):
    for axis, dim in sides:
        count = lax.axis_size(axis)
        forward = [(i, (i + 1) % count) for i in range(count)]
        backward = [(target, source) for source, target in forward]
        size = block.shape[dim]
        low = lax.slice_in_dim(block, 0, width, axis=dim)
        high = lax.slice_in_dim(block, size - width, size, axis=dim)
        from_next = lax.ppermute(low, axis, backward)
        from_prev = lax.ppermute(high, axis, forward)
        head = lax.slice_in_dim(block, width, 2 * width, axis=dim) + from_prev
        middle = lax.slice_in_dim(block, 2 * width, size - 2 * width, axis=dim)
        tail = lax.slice_in_dim(block, size - 2 * width, size - width, axis=dim) + from_next
        block = jnp.concatenate([head, middle, tail], axis=dim)
    return block


def layer_norm(wide_input, gain):
    row_mean = jnp.mean(wide_input, axis=-1, keepdims=True)
    centred = wide_input - row_mean
    variance = jnp.mean(centred * centred, axis=-1, keepdims=True)
    return centred * lax.rsqrt(variance + eps) * gain


def cell_coords(rows, cols, shift):
    row_ids = jnp.arange(rows, dtype=jnp.int32)[:, None] + jnp.zeros((1, cols), jnp.int32) + shift
    col_ids = jnp.arange(cols, dtype=jnp.int32)[None, :] + jnp.zeros((rows, 1), jnp.int32) + shift
    return (row_ids.reshape(-1), col_ids.reshape(-1))


def window_table(query_rows, query_cols, query_shift, key_rows, key_cols, key_shift):
    radius = WIN // 2
    query_i, query_j = cell_coords(query_rows, query_cols, query_shift)
    key_i, key_j = cell_coords(key_rows, key_cols, key_shift)
    offsets = jnp.arange(WIN * WIN, dtype=jnp.int32)
    step_lat = offsets // WIN - radius
    step_lon = offsets % WIN - radius
    match_lat = key_i[None, None, :] - query_i[:, None, None] == step_lat[None, :, None]
    match_lon = key_j[None, None, :] - query_j[:, None, None] == step_lon[None, :, None]
    return match_lat & match_lon


def attend(queries, keys_wide, values_wide, bias, allowed, table_full):
    tile_rows, tile_cols = (queries.shape[0], queries.shape[1])
    score_scale = HEAD_DIM ** (-0.5)
    cells = tile_rows * tile_cols
    query_heads = queries.reshape(cells, HEADS, HEAD_DIM)
    key_heads = keys_wide.reshape(-1, HEADS, HEAD_DIM)
    value_heads = values_wide.reshape(-1, HEADS, HEAD_DIM)
    raw = jnp.einsum("qhd,khd->hqk", query_heads, key_heads, preferred_element_type=jnp.float32)
    bias_dense = jnp.einsum("ho,qok->hqk", bias, table_full, precision=lax.Precision.HIGHEST)
    scores = raw * score_scale + bias_dense
    masked = jnp.where(allowed[None], scores, -jnp.inf)
    row_max = jnp.max(masked, axis=-1, keepdims=True)
    weights_exp = jnp.exp(masked - row_max)
    attention = weights_exp / jnp.sum(weights_exp, axis=-1, keepdims=True)
    probs_low = attention.astype(jnp.bfloat16)
    mixed = jnp.einsum("hqk,khd->qhd", probs_low, value_heads, preferred_element_type=jnp.float32)
    return (
        attention,
        probs_low,
        mixed.reshape(tile_rows, tile_cols, HEADS * HEAD_DIM).astype(jnp.bfloat16),
    )


def pull_back(received, back_table):
    inner_width = HEADS * HEAD_DIM
    spread = HEADS * WIN * WIN
    flat = received.reshape(-1, received.shape[-1])
    query_heads = flat[:, :inner_width].reshape(-1, HEADS, HEAD_DIM)
    grad_heads = flat[:, inner_width : 2 * inner_width].reshape(-1, HEADS, HEAD_DIM)
    prob_piece = flat[:, 2 * inner_width : 2 * inner_width + spread].reshape(-1, HEADS, WIN * WIN)
    score_piece = flat[:, 2 * inner_width + spread :].reshape(-1, HEADS, WIN * WIN)
    score_dense = jnp.einsum(
        "qho,qok->hqk", score_piece, back_table, preferred_element_type=jnp.float32
    ).astype(jnp.bfloat16)
    prob_dense = jnp.einsum(
        "qho,qok->hqk", prob_piece, back_table, preferred_element_type=jnp.float32
    ).astype(jnp.bfloat16)
    grad_keys = jnp.einsum(
        "hqk,qhd->khd", score_dense, query_heads, preferred_element_type=jnp.float32
    )
    grad_values = jnp.einsum(
        "hqk,qhd->khd", prob_dense, grad_heads, preferred_element_type=jnp.float32
    )
    return (grad_keys * HEAD_DIM ** (-0.5), grad_values)


def shards(inputs, input_weight, output_weight, norm_gain, position_bias, cotangent):
    radius = WIN // 2
    inner_width = HEADS * HEAD_DIM
    score_scale = HEAD_DIM ** (-0.5)
    tile_rows, tile_cols = (inputs.shape[0], inputs.shape[1])
    cells = tile_rows * tile_cols
    wide_rows = tile_rows + 2 * radius
    wide_cols = tile_cols + 2 * radius
    first_row = lax.axis_index("lat") * tile_rows - radius
    global_rows = first_row + jnp.arange(wide_rows, dtype=jnp.int32)
    valid_rows = (global_rows >= 0) & (global_rows < tile_rows * lax.axis_size("lat"))
    row_keep = valid_rows.astype(jnp.bfloat16)[:, None, None]
    key_valid = (valid_rows[:, None] & jnp.ones((1, wide_cols), jnp.bool_)).reshape(-1)
    forward_table = window_table(tile_rows, tile_cols, radius, wide_rows, wide_cols, 0)
    table_low = forward_table.astype(jnp.bfloat16)
    table_full = forward_table.astype(jnp.float32)
    query_row = jnp.arange(cells, dtype=jnp.int32) // tile_cols
    query_col = jnp.arange(cells, dtype=jnp.int32) % tile_cols
    key_row = jnp.arange(wide_rows * wide_cols, dtype=jnp.int32) // wide_cols
    key_col = jnp.arange(wide_rows * wide_cols, dtype=jnp.int32) % wide_cols
    step_row = key_row[None, :] - query_row[:, None]
    step_col = key_col[None, :] - query_col[:, None]
    in_window = (step_row >= 0) & (step_row < WIN) & (step_col >= 0) & (step_col < WIN)
    allowed = in_window & key_valid[None, :]
    back_table = window_table(wide_rows, wide_cols, 0, tile_rows, tile_cols, radius).astype(
        jnp.bfloat16
    )
    stream = inputs
    stored = []
    for layer_idx in range(LAYERS):
        wide_input = stream.astype(jnp.float32)
        normed_wide, pullback = jax.vjp(layer_norm, wide_input, norm_gain[layer_idx])
        normed = normed_wide.astype(jnp.bfloat16)
        packed = jnp.einsum(
            "abd,de->abe", normed, input_weight[layer_idx], preferred_element_type=jnp.float32
        ).astype(jnp.bfloat16)
        queries = packed[..., :inner_width]
        key_value = packed[..., inner_width:]
        pair_wide = extended(key_value, (("lat", 0), ("lon", 1)), radius)
        keys_wide = pair_wide[..., :inner_width]
        values_wide = pair_wide[..., inner_width:]
        attention, probs_low, mixed = attend(
            queries, keys_wide, values_wide, position_bias[layer_idx], allowed, table_full
        )
        branch = jnp.einsum(
            "abi,id->abd", mixed, output_weight[layer_idx], preferred_element_type=jnp.float32
        )
        stored.append(
            (pullback, normed, queries, keys_wide, values_wide, attention, probs_low, mixed)
        )
        stream = (wide_input + branch).astype(jnp.bfloat16)
    upstream = cotangent
    packed_terms = [None] * LAYERS
    output_terms = [None] * LAYERS
    gain_terms = [None] * LAYERS
    bias_terms = [None] * LAYERS
    for layer_idx in reversed(range(LAYERS)):
        pullback, normed, queries, keys_wide, values_wide, attention, probs_low, mixed = stored[
            layer_idx
        ]
        output_term = jnp.einsum("abi,abd->id", mixed, upstream, preferred_element_type=jnp.float32)
        output_part = lon_sum(output_term)
        grad_mixed = jnp.einsum(
            "abd,id->abi", upstream, output_weight[layer_idx], preferred_element_type=jnp.float32
        ).astype(jnp.bfloat16)
        grad_heads = grad_mixed.reshape(cells, HEADS, HEAD_DIM)
        key_heads = keys_wide.reshape(-1, HEADS, HEAD_DIM)
        value_heads = values_wide.reshape(-1, HEADS, HEAD_DIM)
        grad_probs = jnp.einsum(
            "qhd,khd->hqk", grad_heads, value_heads, preferred_element_type=jnp.float32
        )
        row_delta = jnp.sum(attention * grad_probs, axis=-1, keepdims=True)
        grad_scores = attention * (grad_probs - row_delta)
        bias_terms[layer_idx] = jnp.einsum(
            "hqk,qok->ho", grad_scores, table_full, precision=lax.Precision.HIGHEST
        )
        scores_low = grad_scores.astype(jnp.bfloat16)
        grad_query = jnp.einsum(
            "hqk,khd->qhd", scores_low, key_heads, preferred_element_type=jnp.float32
        )
        query_rows = queries.reshape(cells, HEADS, HEAD_DIM)
        key_spread = jnp.einsum(
            "hqk,qhd->khd", scores_low, query_rows, preferred_element_type=jnp.float32
        ).reshape(wide_rows, wide_cols, inner_width)
        value_spread = jnp.einsum(
            "hqk,qhd->khd", probs_low, grad_heads, preferred_element_type=jnp.float32
        ).reshape(wide_rows, wide_cols, inner_width)
        spread = jnp.concatenate([key_spread, value_spread], axis=-1)
        spread = jnp.where(valid_rows[:, None, None], spread, 0.0)
        gathered = folded(spread, (("lon", 1), ("lat", 0)), radius)
        grad_keys = gathered[..., :inner_width] * score_scale
        grad_values = gathered[..., inner_width:]
        grad_packed = jnp.concatenate(
            [
                (grad_query * score_scale).reshape(tile_rows, tile_cols, inner_width),
                grad_keys.reshape(tile_rows, tile_cols, inner_width),
                grad_values.reshape(tile_rows, tile_cols, inner_width),
            ],
            axis=-1,
        ).astype(jnp.bfloat16)
        packed_term = jnp.einsum(
            "abd,abe->de", normed, grad_packed, preferred_element_type=jnp.float32
        )
        grad_normed = jnp.einsum(
            "abe,de->abd", grad_packed, input_weight[layer_idx], preferred_element_type=jnp.float32
        )
        grad_wide, gain_term = pullback(grad_normed)
        gain_terms[layer_idx] = gain_term
        upstream = (upstream.astype(jnp.float32) + grad_wide).astype(jnp.bfloat16)
        packed_part = lon_sum(packed_term)
        summed = doubling_sum(jnp.concatenate([output_part, packed_part]), "lat", jnp.bfloat16)
        out_size = output_part.shape[0]
        output_terms[layer_idx] = summed[:out_size].reshape(-1, output_term.shape[1])
        packed_terms[layer_idx] = summed[out_size:].reshape(-1, packed_term.shape[1])
    stats = jnp.concatenate(
        [jnp.stack(gain_terms).reshape(-1), jnp.stack(bias_terms).reshape(-1)]
    )
    stats = doubling_sum(doubling_sum(stats, "lon", jnp.float32), "lat", jnp.float32)
    gain_count = LAYERS * norm_gain.shape[-1]
    gain_grad = stats[:gain_count].reshape(norm_gain.shape)
    bias_grad = stats[gain_count:].reshape(position_bias.shape)
    packed_grad = jnp.stack(packed_terms)
    output_grad = jnp.stack(output_terms)
    return (stream, upstream, packed_grad, output_grad, gain_grad, bias_grad)


def solution(mesh):
    return jax.shard_map(
        shards,
        mesh=mesh,
        in_specs=(P("lat", "lon", None), P(), P(), P(), P(), P("lat", "lon", None)),
        out_specs=(
            P("lat", "lon", None),
            P("lat", "lon", None),
            P(None, "lon", None),
            P(None, "lon", None),
            P(),
            P(),
        ),
        check_vma=False,
    )
```

```python
import jax
import jax.numpy as jnp
from jax import lax
from jax.sharding import PartitionSpec as P

HEADS = 8
HEAD_DIM = 64
WIN = 7
LAYERS = 2


eps = 1e-05


def extended(block, sides, width):
    for axis, dim in sides:
        count = lax.axis_size(axis)
        forward = [(i, i + 1) for i in range(count - 1)]
        forward.append((count - 1, 0))
        backward = [(target, source) for source, target in forward]
        low = lax.ppermute(
            lax.slice_in_dim(block, block.shape[dim] - width, None, axis=dim), axis, forward
        )
        high = lax.ppermute(lax.slice_in_dim(block, 0, width, axis=dim), axis, backward)
        block = jnp.concatenate([low, block, high], axis=dim)
    return block


def lon_sum(rows, extra=None):
    part = lax.psum_scatter(rows.astype(jnp.bfloat16), "lon", scatter_dimension=0, tiled=True)
    return part.reshape(-1)


def doubling_sum(value, axis, keep):
    count = lax.axis_size(axis)
    step = 1
    total = value
    while step < count:
        pairs = [(i, i ^ step) for i in range(count)]
        other = lax.ppermute(total, axis, pairs)
        total = total.astype(jnp.float32) + other.astype(jnp.float32)
        step *= 2
        if step < count:
            total = total.astype(keep)
    return total


def folded(block, sides, width):
    for axis, dim in sides:
        count = lax.axis_size(axis)
        forward = [(i, (i + 1) % count) for i in range(count)]
        backward = [(target, source) for source, target in forward]
        size = block.shape[dim]
        low = lax.slice_in_dim(block, 0, width, axis=dim)
        high = lax.slice_in_dim(block, size - width, size, axis=dim)
        from_next = lax.ppermute(low, axis, backward)
        from_prev = lax.ppermute(high, axis, forward)
        head = lax.slice_in_dim(block, width, 2 * width, axis=dim) + from_prev
        middle = lax.slice_in_dim(block, 2 * width, size - 2 * width, axis=dim)
        tail = lax.slice_in_dim(block, size - 2 * width, size - width, axis=dim) + from_next
        block = jnp.concatenate([head, middle, tail], axis=dim)
    return block


def layer_norm(wide_input, gain):
    row_mean = jnp.mean(wide_input, axis=-1, keepdims=True)
    centred = wide_input - row_mean
    variance = jnp.mean(centred * centred, axis=-1, keepdims=True)
    return centred * lax.rsqrt(variance + eps) * gain


def cell_coords(rows, cols, shift):
    row_ids = jnp.arange(rows, dtype=jnp.int32)[:, None] + jnp.zeros((1, cols), jnp.int32) + shift
    col_ids = jnp.arange(cols, dtype=jnp.int32)[None, :] + jnp.zeros((rows, 1), jnp.int32) + shift
    return (row_ids.reshape(-1), col_ids.reshape(-1))


def window_table(query_rows, query_cols, query_shift, key_rows, key_cols, key_shift):
    radius = WIN // 2
    query_i, query_j = cell_coords(query_rows, query_cols, query_shift)
    key_i, key_j = cell_coords(key_rows, key_cols, key_shift)
    offsets = jnp.arange(WIN * WIN, dtype=jnp.int32)
    step_lat = offsets // WIN - radius
    step_lon = offsets % WIN - radius
    match_lat = key_i[None, None, :] - query_i[:, None, None] == step_lat[None, :, None]
    match_lon = key_j[None, None, :] - query_j[:, None, None] == step_lon[None, :, None]
    return match_lat & match_lon


def attend(queries, keys_wide, values_wide, bias, allowed, table_full):
    tile_rows, tile_cols = (queries.shape[0], queries.shape[1])
    score_scale = HEAD_DIM ** (-0.5)
    cells = tile_rows * tile_cols
    query_heads = queries.reshape(cells, HEADS, HEAD_DIM)
    key_heads = keys_wide.reshape(-1, HEADS, HEAD_DIM)
    value_heads = values_wide.reshape(-1, HEADS, HEAD_DIM)
    raw = jnp.einsum("qhd,khd->hqk", query_heads, key_heads, preferred_element_type=jnp.float32)
    bias_dense = jnp.einsum("ho,qok->hqk", bias, table_full, precision=lax.Precision.HIGHEST)
    scores = raw * score_scale + bias_dense
    masked = jnp.where(allowed[None], scores, -jnp.inf)
    row_max = jnp.max(masked, axis=-1, keepdims=True)
    weights_exp = jnp.exp(masked - row_max)
    attention = weights_exp / jnp.sum(weights_exp, axis=-1, keepdims=True)
    probs_low = attention.astype(jnp.bfloat16)
    mixed = jnp.einsum("hqk,khd->qhd", probs_low, value_heads, preferred_element_type=jnp.float32)
    return (
        attention,
        probs_low,
        mixed.reshape(tile_rows, tile_cols, HEADS * HEAD_DIM).astype(jnp.bfloat16),
    )


def pull_back(received, back_table):
    inner_width = HEADS * HEAD_DIM
    spread = HEADS * WIN * WIN
    flat = received.reshape(-1, received.shape[-1])
    query_heads = flat[:, :inner_width].reshape(-1, HEADS, HEAD_DIM)
    grad_heads = flat[:, inner_width : 2 * inner_width].reshape(-1, HEADS, HEAD_DIM)
    prob_piece = flat[:, 2 * inner_width : 2 * inner_width + spread].reshape(-1, HEADS, WIN * WIN)
    score_piece = flat[:, 2 * inner_width + spread :].reshape(-1, HEADS, WIN * WIN)
    score_dense = jnp.einsum(
        "qho,qok->hqk", score_piece, back_table, preferred_element_type=jnp.float32
    ).astype(jnp.bfloat16)
    prob_dense = jnp.einsum(
        "qho,qok->hqk", prob_piece, back_table, preferred_element_type=jnp.float32
    ).astype(jnp.bfloat16)
    grad_keys = jnp.einsum(
        "hqk,qhd->khd", score_dense, query_heads, preferred_element_type=jnp.float32
    )
    grad_values = jnp.einsum(
        "hqk,qhd->khd", prob_dense, grad_heads, preferred_element_type=jnp.float32
    )
    return (grad_keys * HEAD_DIM ** (-0.5), grad_values)


def shards(inputs, input_weight, output_weight, norm_gain, position_bias, cotangent):
    radius = WIN // 2
    inner_width = HEADS * HEAD_DIM
    score_scale = HEAD_DIM ** (-0.5)
    tile_rows, tile_cols = (inputs.shape[0], inputs.shape[1])
    cells = tile_rows * tile_cols
    wide_rows = tile_rows + 2 * radius
    wide_cols = tile_cols + 2 * radius
    first_row = lax.axis_index("lat") * tile_rows - radius
    global_rows = first_row + jnp.arange(wide_rows, dtype=jnp.int32)
    valid_rows = (global_rows >= 0) & (global_rows < tile_rows * lax.axis_size("lat"))
    row_keep = valid_rows.astype(jnp.bfloat16)[:, None, None]
    key_valid = (valid_rows[:, None] & jnp.ones((1, wide_cols), jnp.bool_)).reshape(-1)
    forward_table = window_table(tile_rows, tile_cols, radius, wide_rows, wide_cols, 0)
    table_low = forward_table.astype(jnp.bfloat16)
    table_full = forward_table.astype(jnp.float32)
    query_row = jnp.arange(cells, dtype=jnp.int32) // tile_cols
    query_col = jnp.arange(cells, dtype=jnp.int32) % tile_cols
    key_row = jnp.arange(wide_rows * wide_cols, dtype=jnp.int32) // wide_cols
    key_col = jnp.arange(wide_rows * wide_cols, dtype=jnp.int32) % wide_cols
    step_row = key_row[None, :] - query_row[:, None]
    step_col = key_col[None, :] - query_col[:, None]
    in_window = (step_row >= 0) & (step_row < WIN) & (step_col >= 0) & (step_col < WIN)
    allowed = in_window & key_valid[None, :]
    back_table = window_table(wide_rows, wide_cols, 0, tile_rows, tile_cols, radius).astype(
        jnp.bfloat16
    )
    stream = inputs
    stored = []
    for layer_idx in range(LAYERS):
        wide_input = stream.astype(jnp.float32)
        normed_wide, pullback = jax.vjp(layer_norm, wide_input, norm_gain[layer_idx])
        normed = normed_wide.astype(jnp.bfloat16)
        packed = jnp.einsum(
            "abd,de->abe", normed, input_weight[layer_idx], preferred_element_type=jnp.float32
        ).astype(jnp.bfloat16)
        queries = packed[..., :inner_width]
        key_value = packed[..., inner_width:]
        pair_wide = extended(key_value, (("lat", 0), ("lon", 1)), radius)
        keys_wide = pair_wide[..., :inner_width]
        values_wide = pair_wide[..., inner_width:]
        attention, probs_low, mixed = attend(
            queries, keys_wide, values_wide, position_bias[layer_idx], allowed, table_full
        )
        branch = jnp.einsum(
            "abi,id->abd", mixed, output_weight[layer_idx], preferred_element_type=jnp.float32
        )
        stored.append(
            (pullback, normed, queries, keys_wide, values_wide, attention, probs_low, mixed)
        )
        stream = (wide_input + branch).astype(jnp.bfloat16)
    upstream = cotangent
    packed_terms = [None] * LAYERS
    output_terms = [None] * LAYERS
    gain_terms = [None] * LAYERS
    bias_terms = [None] * LAYERS
    for layer_idx in reversed(range(LAYERS)):
        pullback, normed, queries, keys_wide, values_wide, attention, probs_low, mixed = stored[
            layer_idx
        ]
        output_term = jnp.einsum("abi,abd->id", mixed, upstream, preferred_element_type=jnp.float32)
        output_part = lon_sum(output_term)
        grad_mixed = jnp.einsum(
            "abd,id->abi", upstream, output_weight[layer_idx], preferred_element_type=jnp.float32
        ).astype(jnp.bfloat16)
        grad_heads = grad_mixed.reshape(cells, HEADS, HEAD_DIM)
        key_heads = keys_wide.reshape(-1, HEADS, HEAD_DIM)
        value_heads = values_wide.reshape(-1, HEADS, HEAD_DIM)
        grad_probs = jnp.einsum(
            "qhd,khd->hqk", grad_heads, value_heads, preferred_element_type=jnp.float32
        )
        row_delta = jnp.sum(attention * grad_probs, axis=-1, keepdims=True)
        grad_scores = attention * (grad_probs - row_delta)
        scores_low = grad_scores.astype(jnp.bfloat16)
        bias_terms[layer_idx] = jnp.einsum(
            "hqk,qok->ho", scores_low, table_low, preferred_element_type=jnp.float32
        )
        grad_query = jnp.einsum(
            "hqk,khd->qhd", scores_low, key_heads, preferred_element_type=jnp.float32
        )
        query_rows = queries.reshape(cells, HEADS, HEAD_DIM)
        key_spread = jnp.einsum(
            "hqk,qhd->khd", scores_low, query_rows, preferred_element_type=jnp.float32
        ).reshape(wide_rows, wide_cols, inner_width)
        value_spread = jnp.einsum(
            "hqk,qhd->khd", probs_low, grad_heads, preferred_element_type=jnp.float32
        ).reshape(wide_rows, wide_cols, inner_width)
        spread = jnp.concatenate([key_spread, value_spread], axis=-1)
        spread = jnp.where(valid_rows[:, None, None], spread, 0.0)
        gathered = folded(spread, (("lon", 1), ("lat", 0)), radius)
        grad_keys = gathered[..., :inner_width] * score_scale
        grad_values = gathered[..., inner_width:]
        grad_packed = jnp.concatenate(
            [
                (grad_query * score_scale).reshape(tile_rows, tile_cols, inner_width),
                grad_keys.reshape(tile_rows, tile_cols, inner_width),
                grad_values.reshape(tile_rows, tile_cols, inner_width),
            ],
            axis=-1,
        ).astype(jnp.bfloat16)
        packed_term = jnp.einsum(
            "abd,abe->de", normed, grad_packed, preferred_element_type=jnp.float32
        )
        grad_normed = jnp.einsum(
            "abe,de->abd", grad_packed, input_weight[layer_idx], preferred_element_type=jnp.float32
        )
        grad_wide, gain_term = pullback(grad_normed)
        gain_terms[layer_idx] = gain_term
        upstream = (upstream.astype(jnp.float32) + grad_wide).astype(jnp.bfloat16)
        packed_part = lon_sum(packed_term)
        summed = doubling_sum(jnp.concatenate([output_part, packed_part]), "lat", jnp.bfloat16)
        out_size = output_part.shape[0]
        output_terms[layer_idx] = summed[:out_size].reshape(-1, output_term.shape[1])
        packed_terms[layer_idx] = summed[out_size:].reshape(-1, packed_term.shape[1])
    stats = jnp.concatenate(
        [jnp.stack(gain_terms).reshape(-1), jnp.stack(bias_terms).reshape(-1)]
    )
    stats = doubling_sum(doubling_sum(stats, "lon", jnp.float32), "lat", jnp.float32)
    gain_count = LAYERS * norm_gain.shape[-1]
    gain_grad = stats[:gain_count].reshape(norm_gain.shape)
    bias_grad = stats[gain_count:].reshape(position_bias.shape)
    packed_grad = jnp.stack(packed_terms)
    output_grad = jnp.stack(output_terms)
    return (stream, upstream, packed_grad, output_grad, gain_grad, bias_grad)


def solution(mesh):
    return jax.shard_map(
        shards,
        mesh=mesh,
        in_specs=(P("lat", "lon", None), P(), P(), P(), P(), P("lat", "lon", None)),
        out_specs=(
            P("lat", "lon", None),
            P("lat", "lon", None),
            P(None, "lon", None),
            P(None, "lon", None),
            P(),
            P(),
        ),
        check_vma=False,
    )
```

```python
import jax
import jax.numpy as jnp
from jax import lax
from jax.sharding import PartitionSpec as P

HEADS = 8
HEAD_DIM = 64
WIN = 7
LAYERS = 2


eps = 1e-05


def extended(block, sides, width):
    for axis, dim in sides:
        count = lax.axis_size(axis)
        forward = [(i, i + 1) for i in range(count - 1)]
        forward.append((count - 1, 0))
        backward = [(target, source) for source, target in forward]
        low = lax.ppermute(
            lax.slice_in_dim(block, block.shape[dim] - width, None, axis=dim), axis, forward
        )
        high = lax.ppermute(lax.slice_in_dim(block, 0, width, axis=dim), axis, backward)
        block = jnp.concatenate([low, block, high], axis=dim)
    return block


def lon_sum(rows, extra=None):
    part = lax.psum_scatter(rows.astype(jnp.bfloat16), "lon", scatter_dimension=0, tiled=True)
    return part.reshape(-1)


def doubling_sum(value, axis, keep):
    count = lax.axis_size(axis)
    step = 1
    total = value
    while step < count:
        pairs = [(i, i ^ step) for i in range(count)]
        other = lax.ppermute(total, axis, pairs)
        total = total.astype(jnp.float32) + other.astype(jnp.float32)
        step *= 2
        if step < count:
            total = total.astype(keep)
    return total


def folded(block, sides, width):
    for axis, dim in sides:
        count = lax.axis_size(axis)
        forward = [(i, (i + 1) % count) for i in range(count)]
        backward = [(target, source) for source, target in forward]
        size = block.shape[dim]
        low = lax.slice_in_dim(block, 0, width, axis=dim)
        high = lax.slice_in_dim(block, size - width, size, axis=dim)
        from_next = lax.ppermute(low, axis, backward)
        from_prev = lax.ppermute(high, axis, forward)
        head = lax.slice_in_dim(block, width, 2 * width, axis=dim) + from_prev
        middle = lax.slice_in_dim(block, 2 * width, size - 2 * width, axis=dim)
        tail = lax.slice_in_dim(block, size - 2 * width, size - width, axis=dim) + from_next
        block = jnp.concatenate([head, middle, tail], axis=dim)
    return block


def layer_norm(wide_input, gain):
    row_mean = jnp.mean(wide_input, axis=-1, keepdims=True)
    centred = wide_input - row_mean
    variance = jnp.mean(centred * centred, axis=-1, keepdims=True)
    return centred * lax.rsqrt(variance + eps) * gain


def cell_coords(rows, cols, shift):
    row_ids = jnp.arange(rows, dtype=jnp.int32)[:, None] + jnp.zeros((1, cols), jnp.int32) + shift
    col_ids = jnp.arange(cols, dtype=jnp.int32)[None, :] + jnp.zeros((rows, 1), jnp.int32) + shift
    return (row_ids.reshape(-1), col_ids.reshape(-1))


def window_table(query_rows, query_cols, query_shift, key_rows, key_cols, key_shift):
    radius = WIN // 2
    query_i, query_j = cell_coords(query_rows, query_cols, query_shift)
    key_i, key_j = cell_coords(key_rows, key_cols, key_shift)
    offsets = jnp.arange(WIN * WIN, dtype=jnp.int32)
    step_lat = offsets // WIN - radius
    step_lon = offsets % WIN - radius
    match_lat = key_i[None, None, :] - query_i[:, None, None] == step_lat[None, :, None]
    match_lon = key_j[None, None, :] - query_j[:, None, None] == step_lon[None, :, None]
    return match_lat & match_lon


def attend(queries, keys_wide, values_wide, bias, allowed, table_full):
    tile_rows, tile_cols = (queries.shape[0], queries.shape[1])
    score_scale = HEAD_DIM ** (-0.5)
    cells = tile_rows * tile_cols
    query_heads = queries.reshape(cells, HEADS, HEAD_DIM)
    key_heads = keys_wide.reshape(-1, HEADS, HEAD_DIM)
    value_heads = values_wide.reshape(-1, HEADS, HEAD_DIM)
    raw = jnp.einsum("qhd,khd->hqk", query_heads, key_heads, preferred_element_type=jnp.float32)
    bias_dense = jnp.einsum("ho,qok->hqk", bias, table_full, precision=lax.Precision.HIGHEST)
    scores = raw * score_scale + bias_dense
    masked = jnp.where(allowed[None], scores, -jnp.inf)
    row_max = jnp.max(masked, axis=-1, keepdims=True)
    weights_exp = jnp.exp(masked - row_max)
    attention = weights_exp / jnp.sum(weights_exp, axis=-1, keepdims=True)
    probs_low = attention.astype(jnp.bfloat16)
    mixed = jnp.einsum("hqk,khd->qhd", probs_low, value_heads, preferred_element_type=jnp.float32)
    return (
        attention,
        probs_low,
        mixed.reshape(tile_rows, tile_cols, HEADS * HEAD_DIM).astype(jnp.bfloat16),
    )


def pull_back(received, back_table):
    inner_width = HEADS * HEAD_DIM
    spread = HEADS * WIN * WIN
    flat = received.reshape(-1, received.shape[-1])
    query_heads = flat[:, :inner_width].reshape(-1, HEADS, HEAD_DIM)
    grad_heads = flat[:, inner_width : 2 * inner_width].reshape(-1, HEADS, HEAD_DIM)
    prob_piece = flat[:, 2 * inner_width : 2 * inner_width + spread].reshape(-1, HEADS, WIN * WIN)
    score_piece = flat[:, 2 * inner_width + spread :].reshape(-1, HEADS, WIN * WIN)
    score_dense = jnp.einsum(
        "qho,qok->hqk", score_piece, back_table, preferred_element_type=jnp.float32
    ).astype(jnp.bfloat16)
    prob_dense = jnp.einsum(
        "qho,qok->hqk", prob_piece, back_table, preferred_element_type=jnp.float32
    ).astype(jnp.bfloat16)
    grad_keys = jnp.einsum(
        "hqk,qhd->khd", score_dense, query_heads, preferred_element_type=jnp.float32
    )
    grad_values = jnp.einsum(
        "hqk,qhd->khd", prob_dense, grad_heads, preferred_element_type=jnp.float32
    )
    return (grad_keys * HEAD_DIM ** (-0.5), grad_values)


def shards(inputs, input_weight, output_weight, norm_gain, position_bias, cotangent):
    radius = WIN // 2
    inner_width = HEADS * HEAD_DIM
    score_scale = HEAD_DIM ** (-0.5)
    tile_rows, tile_cols = (inputs.shape[0], inputs.shape[1])
    cells = tile_rows * tile_cols
    wide_rows = tile_rows + 2 * radius
    wide_cols = tile_cols + 2 * radius
    first_row = lax.axis_index("lat") * tile_rows - radius
    global_rows = first_row + jnp.arange(wide_rows, dtype=jnp.int32)
    valid_rows = (global_rows >= 0) & (global_rows < tile_rows * lax.axis_size("lat"))
    row_keep = valid_rows.astype(jnp.bfloat16)[:, None, None]
    key_valid = (valid_rows[:, None] & jnp.ones((1, wide_cols), jnp.bool_)).reshape(-1)
    forward_table = window_table(tile_rows, tile_cols, radius, wide_rows, wide_cols, 0)
    table_low = forward_table.astype(jnp.bfloat16)
    table_full = forward_table.astype(jnp.float32)
    query_row = jnp.arange(cells, dtype=jnp.int32) // tile_cols
    query_col = jnp.arange(cells, dtype=jnp.int32) % tile_cols
    key_row = jnp.arange(wide_rows * wide_cols, dtype=jnp.int32) // wide_cols
    key_col = jnp.arange(wide_rows * wide_cols, dtype=jnp.int32) % wide_cols
    step_row = key_row[None, :] - query_row[:, None]
    step_col = key_col[None, :] - query_col[:, None]
    in_window = (step_row >= 0) & (step_row < WIN) & (step_col >= 0) & (step_col < WIN)
    allowed = in_window & key_valid[None, :]
    back_table = window_table(wide_rows, wide_cols, 0, tile_rows, tile_cols, radius).astype(
        jnp.bfloat16
    )
    stream = inputs
    stored = []
    for layer_idx in range(LAYERS):
        wide_input = stream.astype(jnp.float32)
        normed_wide, pullback = jax.vjp(layer_norm, wide_input, norm_gain[layer_idx])
        normed = normed_wide.astype(jnp.bfloat16)
        packed = jnp.einsum(
            "abd,de->abe", normed, input_weight[layer_idx], preferred_element_type=jnp.float32
        ).astype(jnp.bfloat16)
        queries = packed[..., :inner_width]
        key_value = packed[..., inner_width:]
        pair_wide = extended(key_value, (("lat", 0), ("lon", 1)), radius)
        keys_wide = pair_wide[..., :inner_width]
        values_wide = pair_wide[..., inner_width:]
        attention, probs_low, mixed = attend(
            queries, keys_wide, values_wide, position_bias[layer_idx], allowed, table_full
        )
        branch = jnp.einsum(
            "abi,id->abd", mixed, output_weight[layer_idx], preferred_element_type=jnp.float32
        )
        stored.append(
            (pullback, normed, queries, keys_wide, values_wide, attention, probs_low, mixed)
        )
        stream = (wide_input + branch).astype(jnp.bfloat16)
    upstream = cotangent
    pending = None
    packed_terms = [None] * LAYERS
    output_terms = [None] * LAYERS
    gain_terms = [None] * LAYERS
    bias_terms = [None] * LAYERS
    for layer_idx in reversed(range(LAYERS)):
        pullback, normed, queries, keys_wide, values_wide, attention, probs_low, mixed = stored[
            layer_idx
        ]
        output_term = jnp.einsum("abi,abd->id", mixed, upstream, preferred_element_type=jnp.float32)
        if pending is not None:
            prev_idx, prev_packed, prev_out = pending
            count = lax.axis_size("lon")
            rows_o = prev_out.shape[0] // count
            both_out = jnp.concatenate(
                [
                    prev_out.astype(jnp.bfloat16).reshape(count, rows_o, -1),
                    output_term.astype(jnp.bfloat16).reshape(count, rows_o, -1),
                ],
                axis=1,
            )
            merged = jnp.concatenate(
                [prev_packed.astype(jnp.bfloat16).reshape(count, 2 * rows_o, -1), both_out], axis=-1
            )
            part = lax.psum_scatter(merged, "lon", scatter_dimension=0, tiled=True)[0]
            width = prev_packed.shape[1]
            prev_packed_part = part[:, :width].reshape(-1)
            prev_out_part = part[:rows_o, width:].reshape(-1)
            output_part = part[rows_o:, width:].reshape(-1)
            summed = doubling_sum(
                jnp.concatenate([prev_out_part, prev_packed_part]), "lat", jnp.bfloat16
            )
            out_size = prev_out_part.shape[0]
            output_terms[prev_idx] = summed[:out_size].reshape(-1, prev_out.shape[1])
            packed_terms[prev_idx] = summed[out_size:].reshape(-1, prev_packed.shape[1])
        grad_mixed = jnp.einsum(
            "abd,id->abi", upstream, output_weight[layer_idx], preferred_element_type=jnp.float32
        ).astype(jnp.bfloat16)
        grad_heads = grad_mixed.reshape(cells, HEADS, HEAD_DIM)
        key_heads = keys_wide.reshape(-1, HEADS, HEAD_DIM)
        value_heads = values_wide.reshape(-1, HEADS, HEAD_DIM)
        grad_probs = jnp.einsum(
            "qhd,khd->hqk", grad_heads, value_heads, preferred_element_type=jnp.float32
        )
        row_delta = jnp.sum(attention * grad_probs, axis=-1, keepdims=True)
        grad_scores = attention * (grad_probs - row_delta)
        scores_low = grad_scores.astype(jnp.bfloat16)
        bias_terms[layer_idx] = jnp.einsum(
            "hqk,qok->ho", scores_low, table_low, preferred_element_type=jnp.float32
        )
        grad_query = jnp.einsum(
            "hqk,khd->qhd", scores_low, key_heads, preferred_element_type=jnp.float32
        )
        query_rows = queries.reshape(cells, HEADS, HEAD_DIM)
        key_spread = jnp.einsum(
            "hqk,qhd->khd", scores_low, query_rows, preferred_element_type=jnp.float32
        ).reshape(wide_rows, wide_cols, inner_width)
        value_spread = jnp.einsum(
            "hqk,qhd->khd", probs_low, grad_heads, preferred_element_type=jnp.float32
        ).reshape(wide_rows, wide_cols, inner_width)
        spread = jnp.concatenate([key_spread, value_spread], axis=-1)
        spread = jnp.where(valid_rows[:, None, None], spread, 0.0)
        gathered = folded(spread, (("lon", 1), ("lat", 0)), radius)
        grad_keys = gathered[..., :inner_width] * score_scale
        grad_values = gathered[..., inner_width:]
        grad_packed = jnp.concatenate(
            [
                (grad_query * score_scale).reshape(tile_rows, tile_cols, inner_width),
                grad_keys.reshape(tile_rows, tile_cols, inner_width),
                grad_values.reshape(tile_rows, tile_cols, inner_width),
            ],
            axis=-1,
        ).astype(jnp.bfloat16)
        packed_term = jnp.einsum(
            "abd,abe->de", normed, grad_packed, preferred_element_type=jnp.float32
        )
        grad_normed = jnp.einsum(
            "abe,de->abd", grad_packed, input_weight[layer_idx], preferred_element_type=jnp.float32
        )
        grad_wide, gain_term = pullback(grad_normed)
        gain_terms[layer_idx] = gain_term
        upstream = (upstream.astype(jnp.float32) + grad_wide).astype(jnp.bfloat16)
        if layer_idx > 0:
            pending = (layer_idx, packed_term, output_term)
        else:
            packed_part = lon_sum(packed_term)
            summed = doubling_sum(jnp.concatenate([output_part, packed_part]), "lat", jnp.bfloat16)
            out_size = output_part.shape[0]
            output_terms[layer_idx] = summed[:out_size].reshape(-1, output_term.shape[1])
            packed_terms[layer_idx] = summed[out_size:].reshape(-1, packed_term.shape[1])
    stats = jnp.concatenate(
        [jnp.stack(gain_terms).reshape(-1), jnp.stack(bias_terms).reshape(-1)]
    )
    stats = doubling_sum(doubling_sum(stats, "lon", jnp.float32), "lat", jnp.float32)
    gain_count = LAYERS * norm_gain.shape[-1]
    gain_grad = stats[:gain_count].reshape(norm_gain.shape)
    bias_grad = stats[gain_count:].reshape(position_bias.shape)
    packed_grad = jnp.stack(packed_terms)
    output_grad = jnp.stack(output_terms)
    return (stream, upstream, packed_grad, output_grad, gain_grad, bias_grad)


def solution(mesh):
    return jax.shard_map(
        shards,
        mesh=mesh,
        in_specs=(P("lat", "lon", None), P(), P(), P(), P(), P("lat", "lon", None)),
        out_specs=(
            P("lat", "lon", None),
            P("lat", "lon", None),
            P(None, "lon", None),
            P(None, "lon", None),
            P(),
            P(),
        ),
        check_vma=False,
    )
```
